128 devices in a mesh: aux: 8 (over y, core), occ: 16 (over x, z).
Axes of the slice: x: 4, y: 4, z: 4, core: 2. Of those that a mesh axis runs over, the one named last changes fastest.
Arguments:
- three_center: bfloat16 [1536, 64, 8192], P('occ', None, 'aux'), may hold values from -0.5 to 0.5
- coefficients: bfloat16 [1536, 64, 64], P('occ'), may hold values from -0.75 to 0.75
- target: int32 [1536], P('occ'), may hold values from 0 to 63, as said below
- domain_slot: int32 [1536], P('occ'), may hold values from 0 to 15
- owner_order: int32 [64], replicated, may hold values from 0 to 63, each once
Outputs:
- exchange_tiles: float32 [1024, 64, 1024], P('aux', 'occ')
The draws below stay inside these ranges and needn't reach their ends.
Inputs may be any that keep to these rules, and one draw needn't show every extreme that they name: `target`: among the 96 tiles of one index of occ, at most 2 name the same occupied tile; some occupied tiles are named exactly 2 times by every index of occ. `owner_order`: each occupied tile appears exactly once.
All inputs are finite; a program needn't handle non-finite values.
Results may differ from the reference program's by a relative error of at most 0.0015.
Values may be sent and summed in bfloat16 or wider, within the bound.
No kernel may reach another device: no remote copies, remote signals or barrier semaphores. Data moves between devices by JAX's collectives and lax.ppermute only.
A program may use at most 192 MiB of HBM per device.

```python
import jax
import jax.numpy as jnp
from jax import lax

TILE = 64
NAUX = 128
DOM = 16
CAP = 2
PAIR_DEV = 96
PA = 16
NOT = 64
NPAIRS = 1536
N_AUX = 8


def draw_target(key, part):
    device_total = NPAIRS // PAIR_DEV
    hot_count = max(1, PAIR_DEV // (4 * CAP))
    key_hot, key_dev = jax.random.split(jax.random.fold_in(key, 11))
    ranking = jnp.argsort(jax.random.permutation(key_hot, NOT))
    hot_flag = (ranking < hot_count).astype(jnp.int32)
    slot_ids = jnp.arange(NOT * CAP, dtype=jnp.int32)
    tile_of = slot_ids // CAP

    def one_device(dev_key):
        key_score, key_order = jax.random.split(dev_key)
        scores = jax.random.randint(key_score, (NOT * CAP,), 0, 2 ** 20, dtype=jnp.int32)
        scores = (scores + hot_flag[tile_of] * 2 ** 20) * (NOT * CAP) + slot_ids
        unused, chosen = lax.top_k(scores, PAIR_DEV)
        picked = tile_of[chosen]
        return picked[jax.random.permutation(key_order, PAIR_DEV)]
    dev_keys = jax.random.split(key_dev, device_total)
    return jax.vmap(one_device)(dev_keys).reshape(NPAIRS).astype(jnp.int32)


def touch_ends(drawn, stream_key, least, high):
    shape = drawn.shape
    spot = [jax.random.randint(jax.random.fold_in(stream_key, axis), (), 0, shape[axis]) for axis in range(len(shape))]
    drawn = drawn.at[tuple(spot)].set(least)
    longest = shape.index(max(shape))
    spot[longest] = (spot[longest] + 1) % shape[longest]
    return drawn.at[tuple(spot)].set(high)


def level_of(rng, dims, shards, low, high):
    factor_of, own = 1.0, jax.random.fold_in(rng, 6)
    for position, blocks in shards:
        heights = jnp.exp(jax.random.uniform(jax.random.fold_in(own, position), (blocks,), jnp.float32, low / len(shards), high / len(shards)))
        factor_of = factor_of * jnp.repeat(heights, dims[position] // blocks).reshape([-1 if axis == position else 1 for axis in range(len(dims))])
    return factor_of


def noise(key, extent, spread, reach, shards=(), held_as=jnp.bfloat16):
    factor_of = level_of(key, extent, shards, -0.22, 0.18) if shards else 1.0
    drawn = jax.random.normal(key, extent, jnp.float32) * spread * factor_of
    return jnp.minimum(jnp.maximum(drawn, -reach), reach).astype(held_as)


def setup_inputs(seed: int = 0) -> dict:
    seeds = jax.random.split(jax.random.key(seed), 6)
    three_center = noise(seeds[0], (NPAIRS, TILE, NAUX * TILE), ((NAUX * TILE) ** -0.375), 0.5, ((0, 16), (2, 8)))
    coefficients = noise(seeds[1], (NPAIRS, TILE, TILE), TILE ** -0.5, 0.75, ((0, 16),))
    target = draw_target(jax.random.fold_in(seeds[5], 71), 0)
    domain_slot = touch_ends(jax.random.randint(seeds[3], (NPAIRS,), 0, DOM), jax.random.fold_in(seeds[3], 1), 0, DOM - 1).astype(jnp.int32)
    owner_order = jax.random.permutation(seeds[4], NOT).astype(jnp.int32)
    return {"three_center": three_center, "coefficients": coefficients, "target": target, "domain_slot": domain_slot, "owner_order": owner_order}


def reference(three_center, coefficients, target, domain_slot, owner_order):
    pair_total = three_center.shape[0]
    col_width = PA * TILE
    domain_rows = DOM * TILE
    segment_ids = (target * DOM + domain_slot).astype(jnp.int32)
    coef_wide = coefficients.astype(jnp.float32)

    def add_group(group_index, running):
        start_col = (group_index * col_width).astype(jnp.int32)
        aux_slice = lax.dynamic_slice_in_dim(three_center, start_col, col_width, 2).astype(jnp.float32)
        blocks = jnp.einsum("pmav,pvi->pmai", aux_slice.reshape(pair_total, TILE, PA, TILE), coef_wide)
        blocks = lax.optimization_barrier(blocks.astype(jnp.bfloat16)).astype(jnp.float32)
        blocks = blocks.reshape(pair_total, TILE, col_width)
        fitted = jax.ops.segment_sum(blocks, segment_ids, NOT * DOM).astype(jnp.bfloat16)
        fitted = lax.optimization_barrier(fitted).astype(jnp.float32).reshape(NOT, domain_rows, col_width)
        partial_gram = jnp.einsum("trw,tcw->rtc", fitted, fitted)
        return running + partial_gram

    total = lax.fori_loop(0, N_AUX, add_group, jnp.zeros((domain_rows, NOT, domain_rows), jnp.float32))
    return jnp.take(total, owner_order.astype(jnp.int32), axis=1)
```

```python
import math

import jax
import jax.numpy as jnp
from jax import lax
from jax.experimental import pallas as pl
from jax.experimental.pallas import tpu as pltpu
from jax.sharding import PartitionSpec as P

DOM = 16
CAP = 2
LANES = 256


def _transform_kernel(slot_ref, empty_ref, tc_ref, w_ref, out_hbm, buf, zero, sems):
    step = pl.program_id(0)
    steps = pl.num_programs(0)
    per = tc_ref.shape[0]
    epr = sems.shape[1] - per
    rows, width = tc_ref.shape[1], tc_ref.shape[2]
    groups = width // LANES
    half = w_ref.shape[1]
    side = buf.at[step % 2]

    @pl.when(step == 0)
    def _():
        zero[...] = jnp.zeros_like(zero)

    def copies(at, parity):
        held = buf.at[parity]
        out = [
            pltpu.make_async_copy(held.at[j], out_hbm.at[slot_ref[at * per + j]], sems.at[parity, j])
            for j in range(per)
        ]
        out += [
            pltpu.make_async_copy(zero, out_hbm.at[empty_ref[at * epr + j]], sems.at[parity, per + j])
            for j in range(epr)
        ]
        return out

    @pl.when(step >= 2)
    def _():
        for cp in copies(step - 2, step % 2):
            cp.wait()

    pad = jnp.zeros((half, half), w_ref.dtype)
    for j in range(per):
        w2 = w_ref[j]
        w4 = jnp.concatenate(
            [jnp.concatenate([w2, pad], axis=1), jnp.concatenate([pad, w2], axis=1)], axis=0
        )
        x = tc_ref[j]
        stacked = jnp.concatenate([x[:, g * LANES:(g + 1) * LANES] for g in range(groups)], axis=0)
        y = jnp.dot(stacked, w4, preferred_element_type=jnp.float32).astype(buf.dtype)
        for g in range(groups):
            side[j, :, g * LANES:(g + 1) * LANES] = y[g * rows:(g + 1) * rows]

    for cp in copies(step, step % 2):
        cp.start()

    @pl.when(step == steps - 1)
    def _():
        for cp in copies(step - 1, (step + 1) % 2):
            cp.wait()
        for cp in copies(step, step % 2):
            cp.wait()


def transform_into_slots(three_center, coefficients, buffer_slot, empty_slot, slot_count):
    pair_count, rows, width = three_center.shape
    tile = coefficients.shape[1]
    empty_count = empty_slot.shape[0]
    steps = math.gcd(pair_count, empty_count)
    steps = 8 if steps % 8 == 0 else steps
    per = pair_count // steps
    epr = empty_count // steps
    zeros = jnp.zeros_like(coefficients)
    w2 = jnp.concatenate(
        [
            jnp.concatenate([coefficients, zeros], axis=2),
            jnp.concatenate([zeros, coefficients], axis=2),
        ],
        axis=1,
    )
    grid_spec = pltpu.PrefetchScalarGridSpec(
        num_scalar_prefetch=2,
        grid=(steps,),
        in_specs=[
            pl.BlockSpec((per, rows, width), lambda i, s, e: (i, 0, 0)),
            pl.BlockSpec((per, 2 * tile, 2 * tile), lambda i, s, e: (i, 0, 0)),
        ],
        out_specs=pl.BlockSpec(memory_space=pl.ANY),
        scratch_shapes=[
            pltpu.VMEM((2, per, rows, width), three_center.dtype),
            pltpu.VMEM((rows, width), three_center.dtype),
            pltpu.SemaphoreType.DMA((2, per + epr)),
        ],
    )
    block_bytes = rows * width * 2
    return pl.pallas_call(
        _transform_kernel,
        grid_spec=grid_spec,
        out_shape=jax.ShapeDtypeStruct((slot_count, rows, width), three_center.dtype),
        compiler_params=pltpu.CompilerParams(dimension_semantics=("arbitrary",)),
        cost_estimate=pl.CostEstimate(
            flops=2 * pair_count * rows * width * 4 * tile,
            transcendentals=0,
            bytes_accessed=(pair_count + slot_count) * block_bytes,
        ),
    )(buffer_slot, empty_slot, three_center, w2)


def _gram_kernel(lab_ref, x_ref, o_ref, acc):
    k = pl.program_id(0)
    sources, cap = x_ref.shape[0], x_ref.shape[1]
    per_source = lab_ref.shape[0] // sources
    acc[...] = jnp.zeros_like(acc)
    for s in range(sources):
        for c in range(cap):
            e = lab_ref[s * per_source + k * cap + c]

            @pl.when(e >= 0)
            def _():
                acc[e] += x_ref[s, c].astype(jnp.float32)

    dom, rows, width = acc.shape
    fitted = acc[...].astype(x_ref.dtype).reshape(dom * rows, width)
    o_ref[...] = lax.dot_general(
        fitted, fitted, (((1,), (1,)), ((), ())), preferred_element_type=jnp.float32
    )


def domain_gram(received, labels, dom):
    sources, slots, rows, width = received.shape
    owned = slots // CAP
    domain_rows = dom * rows
    grid_spec = pltpu.PrefetchScalarGridSpec(
        num_scalar_prefetch=1,
        grid=(owned,),
        in_specs=[pl.BlockSpec((sources, CAP, rows, width), lambda k, lab: (0, k, 0, 0))],
        out_specs=pl.BlockSpec((domain_rows, domain_rows), lambda k, lab: (0, k)),
        scratch_shapes=[pltpu.VMEM((dom, rows, width), jnp.float32)],
    )
    return pl.pallas_call(
        _gram_kernel,
        grid_spec=grid_spec,
        out_shape=jax.ShapeDtypeStruct((domain_rows, owned * domain_rows), jnp.float32),
        compiler_params=pltpu.CompilerParams(
            dimension_semantics=("arbitrary",), vmem_limit_bytes=60 * 1024 * 1024
        ),
        cost_estimate=pl.CostEstimate(
            flops=2 * owned * domain_rows * domain_rows * width,
            transcendentals=0,
            bytes_accessed=sources * slots * rows * width * 2 + owned * domain_rows * domain_rows * 4,
        ),
    )(labels.reshape(-1), received)


def per_device(three_center, coefficients, target, domain_slot, owner_order):
    pair_count, tile_width, col_width = three_center.shape
    occ_count = lax.axis_size("occ")
    tile_count = owner_order.shape[0]
    owned_tiles = tile_count // occ_count
    slot_count = tile_count * CAP
    tile_ids = jnp.arange(tile_count, dtype=jnp.int32)
    position = jnp.sum(
        jnp.where(owner_order[None, :] == tile_ids[:, None], tile_ids[None, :], 0), axis=1
    )
    pair_ids = jnp.arange(pair_count, dtype=jnp.int32)
    earlier = (target[:, None] == target[None, :]) & (pair_ids[:, None] > pair_ids[None, :])
    buffer_slot = jnp.take(position, target) * CAP + jnp.sum(earlier.astype(jnp.int32), axis=1)
    labels = jnp.full((slot_count,), -1, jnp.int32).at[buffer_slot].set(domain_slot)
    empty_count = slot_count - pair_count
    empty_slot = jnp.nonzero(labels < 0, size=empty_count, fill_value=0)[0].astype(jnp.int32)
    labels = labels.reshape(occ_count, owned_tiles * CAP)

    buffer = transform_into_slots(three_center, coefficients, buffer_slot, empty_slot, slot_count)
    buffer = buffer.reshape(occ_count, owned_tiles * CAP * tile_width, col_width)
    received = lax.all_to_all(buffer, "occ", split_axis=0, concat_axis=0, tiled=True)
    received_labels = lax.all_to_all(labels, "occ", split_axis=0, concat_axis=0, tiled=True)
    received = received.reshape(occ_count, owned_tiles * CAP, tile_width, col_width)

    partial_gram = domain_gram(received, received_labels, DOM)
    domain_rows = partial_gram.shape[0]
    summed = lax.psum_scatter(partial_gram, "aux", scatter_dimension=0, tiled=True)
    return summed.reshape(summed.shape[0], owned_tiles, domain_rows)


def solution(mesh):
    in_specs = (P("occ", None, "aux"), P("occ", None, None), P("occ"), P("occ"), P())
    out_specs = P("aux", "occ", None)
    return jax.shard_map(
        per_device, mesh=mesh, in_specs=in_specs, out_specs=out_specs, check_vma=False
    )
```

```python
import math

import jax
import jax.numpy as jnp
from jax import lax
from jax.experimental import pallas as pl
from jax.experimental.pallas import tpu as pltpu
from jax.sharding import PartitionSpec as P

DOM = 16
CAP = 2
LANES = 256


def _transform_kernel(slot_ref, empty_ref, tc_ref, w_ref, *rest):
    chunks = (len(rest) - 3)
    outs, (buf, zero, sems) = rest[:chunks], rest[chunks:]
    chunk_slots = outs[0].shape[0]
    step = pl.program_id(0)
    steps = pl.num_programs(0)
    per = tc_ref.shape[0]
    epr = sems.shape[1] - per
    rows, width = tc_ref.shape[1], tc_ref.shape[2]
    groups = width // LANES
    half = w_ref.shape[1]
    side = buf.at[step % 2]

    @pl.when(step == 0)
    def _():
        zero[...] = jnp.zeros_like(zero)

    def each_copy(at, parity, act):
        held = buf.at[parity]
        for j in range(per + epr):
            if j < per:
                src, g = held.at[j], slot_ref[at * per + j]
            else:
                src, g = zero, empty_ref[at * epr + j - per]
            chunk, local = g // chunk_slots, g % chunk_slots
            for kk in range(chunks):
                @pl.when(chunk == kk)
                def _():
                    act(pltpu.make_async_copy(src, outs[kk].at[local], sems.at[parity, j]))

    def start(cp):
        cp.start()

    def wait(cp):
        cp.wait()

    @pl.when(step >= 2)
    def _():
        each_copy(step - 2, step % 2, wait)

    pad = jnp.zeros((half, half), w_ref.dtype)
    for j in range(per):
        w2 = w_ref[j]
        w4 = jnp.concatenate(
            [jnp.concatenate([w2, pad], axis=1), jnp.concatenate([pad, w2], axis=1)], axis=0
        )
        x = tc_ref[j]
        stacked = jnp.concatenate([x[:, g * LANES:(g + 1) * LANES] for g in range(groups)], axis=0)
        y = jnp.dot(stacked, w4, preferred_element_type=jnp.float32).astype(buf.dtype)
        for g in range(groups):
            side[j, :, g * LANES:(g + 1) * LANES] = y[g * rows:(g + 1) * rows]

    each_copy(step, step % 2, start)

    @pl.when(step == steps - 1)
    def _():
        each_copy(step - 1, (step + 1) % 2, wait)
        each_copy(step, step % 2, wait)


def transform_into_slots(three_center, coefficients, buffer_slot, empty_slot, slot_count, chunks):
    pair_count, rows, width = three_center.shape
    tile = coefficients.shape[1]
    empty_count = empty_slot.shape[0]
    steps = math.gcd(pair_count, empty_count)
    steps = 8 if steps % 8 == 0 else steps
    per = pair_count // steps
    epr = empty_count // steps
    zeros = jnp.zeros_like(coefficients)
    w2 = jnp.concatenate(
        [
            jnp.concatenate([coefficients, zeros], axis=2),
            jnp.concatenate([zeros, coefficients], axis=2),
        ],
        axis=1,
    )
    grid_spec = pltpu.PrefetchScalarGridSpec(
        num_scalar_prefetch=2,
        grid=(steps,),
        in_specs=[
            pl.BlockSpec((per, rows, width), lambda i, s, e: (i, 0, 0)),
            pl.BlockSpec((per, 2 * tile, 2 * tile), lambda i, s, e: (i, 0, 0)),
        ],
        out_specs=[pl.BlockSpec(memory_space=pl.ANY)] * chunks,
        scratch_shapes=[
            pltpu.VMEM((2, per, rows, width), three_center.dtype),
            pltpu.VMEM((rows, width), three_center.dtype),
            pltpu.SemaphoreType.DMA((2, per + epr)),
        ],
    )
    block_bytes = rows * width * 2
    chunk_shape = jax.ShapeDtypeStruct((slot_count // chunks, rows, width), three_center.dtype)
    return pl.pallas_call(
        _transform_kernel,
        grid_spec=grid_spec,
        out_shape=[chunk_shape] * chunks,
        compiler_params=pltpu.CompilerParams(dimension_semantics=("arbitrary",)),
        cost_estimate=pl.CostEstimate(
            flops=2 * pair_count * rows * width * 4 * tile,
            transcendentals=0,
            bytes_accessed=(pair_count + slot_count) * block_bytes,
        ),
    )(buffer_slot, empty_slot, three_center, w2)


def _gram_kernel(lab_ref, x_ref, o_ref, acc):
    k = pl.program_id(0)
    sources, cap = x_ref.shape[0], x_ref.shape[1]
    per_source = lab_ref.shape[0] // sources
    acc[...] = jnp.zeros_like(acc)
    for s in range(sources):
        for c in range(cap):
            e = lab_ref[s * per_source + k * cap + c]

            @pl.when(e >= 0)
            def _():
                acc[e] += x_ref[s, c].astype(jnp.float32)

    dom, rows, width = acc.shape
    fitted = acc[...].astype(x_ref.dtype).reshape(dom * rows, width)
    o_ref[...] = lax.dot_general(
        fitted, fitted, (((1,), (1,)), ((), ())), preferred_element_type=jnp.float32
    )


def domain_gram(received, labels, dom):
    sources, slots, rows, width = received.shape
    owned = slots // CAP
    domain_rows = dom * rows
    grid_spec = pltpu.PrefetchScalarGridSpec(
        num_scalar_prefetch=1,
        grid=(owned,),
        in_specs=[pl.BlockSpec((sources, CAP, rows, width), lambda k, lab: (0, k, 0, 0))],
        out_specs=pl.BlockSpec((domain_rows, domain_rows), lambda k, lab: (0, k)),
        scratch_shapes=[pltpu.VMEM((dom, rows, width), jnp.float32)],
    )
    return pl.pallas_call(
        _gram_kernel,
        grid_spec=grid_spec,
        out_shape=jax.ShapeDtypeStruct((domain_rows, owned * domain_rows), jnp.float32),
        compiler_params=pltpu.CompilerParams(
            dimension_semantics=("arbitrary",), vmem_limit_bytes=60 * 1024 * 1024
        ),
        cost_estimate=pl.CostEstimate(
            flops=2 * owned * domain_rows * domain_rows * width,
            transcendentals=0,
            bytes_accessed=sources * slots * rows * width * 2 + owned * domain_rows * domain_rows * 4,
        ),
    )(labels.reshape(-1), received)


def per_device(three_center, coefficients, target, domain_slot, owner_order):
    pair_count, tile_width, col_width = three_center.shape
    occ_count = lax.axis_size("occ")
    tile_count = owner_order.shape[0]
    owned_tiles = tile_count // occ_count
    slot_count = tile_count * CAP
    tile_ids = jnp.arange(tile_count, dtype=jnp.int32)
    position = jnp.sum(
        jnp.where(owner_order[None, :] == tile_ids[:, None], tile_ids[None, :], 0), axis=1
    )
    pair_ids = jnp.arange(pair_count, dtype=jnp.int32)
    earlier = (target[:, None] == target[None, :]) & (pair_ids[:, None] > pair_ids[None, :])
    rank = jnp.sum(earlier.astype(jnp.int32), axis=1)
    pos = jnp.take(position, target)
    buffer_slot = ((pos % owned_tiles) * occ_count + pos // owned_tiles) * CAP + rank
    labels = jnp.full((slot_count,), -1, jnp.int32).at[buffer_slot].set(domain_slot)
    empty_count = slot_count - pair_count
    empty_slot = jnp.nonzero(labels < 0, size=empty_count, fill_value=0)[0].astype(jnp.int32)
    labels = labels.reshape(owned_tiles, occ_count, CAP).transpose(1, 0, 2)
    received_labels = lax.all_to_all(labels, "occ", split_axis=0, concat_axis=0, tiled=True)

    buffers = transform_into_slots(
        three_center, coefficients, buffer_slot, empty_slot, slot_count, owned_tiles
    )
    pieces = []
    for k in range(owned_tiles):
        buffer = buffers[k].reshape(occ_count, CAP * tile_width, col_width)
        received = lax.all_to_all(buffer, "occ", split_axis=0, concat_axis=0, tiled=True)
        received = received.reshape(occ_count, CAP, tile_width, col_width)
        partial_gram = domain_gram(received, received_labels[:, k], DOM)
        pieces.append(lax.psum_scatter(partial_gram, "aux", scatter_dimension=0, tiled=True))
    return jnp.stack(pieces, axis=1)


def solution(mesh):
    in_specs = (P("occ", None, "aux"), P("occ", None, None), P("occ"), P("occ"), P())
    out_specs = P("aux", "occ", None)
    return jax.shard_map(
        per_device, mesh=mesh, in_specs=in_specs, out_specs=out_specs, check_vma=False
    )
```

```python
import math

import jax
import jax.numpy as jnp
from jax import lax
from jax.experimental import pallas as pl
from jax.experimental.pallas import tpu as pltpu
from jax.sharding import PartitionSpec as P

DOM = 16
CAP = 2
LANES = 256


def _transform_kernel(out_ref, slot_ref, tc_ref, w_ref, *rest):
    chunks = len(rest) - 2
    outs, (buf, sems) = rest[:chunks], rest[chunks:]
    step = pl.program_id(0)
    steps = pl.num_programs(0)
    per = tc_ref.shape[0]
    rows, width = tc_ref.shape[1], tc_ref.shape[2]
    groups = width // LANES
    half = w_ref.shape[1]
    side = buf.at[step % 2]

    def each_copy(at, parity, act):
        held = buf.at[parity]
        for j in range(per):
            chunk, local = out_ref[at * per + j], slot_ref[at * per + j]
            for kk in range(chunks):
                @pl.when(chunk == kk)
                def _():
                    act(pltpu.make_async_copy(held.at[j], outs[kk].at[local], sems.at[parity, j]))

    def start(cp):
        cp.start()

    def wait(cp):
        cp.wait()

    @pl.when(step >= 2)
    def _():
        each_copy(step - 2, step % 2, wait)

    pad = jnp.zeros((half, half), w_ref.dtype)
    for j in range(per):
        w2 = w_ref[j]
        w4 = jnp.concatenate(
            [jnp.concatenate([w2, pad], axis=1), jnp.concatenate([pad, w2], axis=1)], axis=0
        )
        x = tc_ref[j]
        stacked = jnp.concatenate([x[:, g * LANES:(g + 1) * LANES] for g in range(groups)], axis=0)
        y = jnp.dot(stacked, w4, preferred_element_type=jnp.float32).astype(buf.dtype)
        for g in range(groups):
            side[j, :, g * LANES:(g + 1) * LANES] = y[g * rows:(g + 1) * rows]

    each_copy(step, step % 2, start)

    @pl.when(step == steps - 1)
    def _():
        each_copy(step - 1, (step + 1) % 2, wait)
        each_copy(step, step % 2, wait)


def transform_into_slots(three_center, coefficients, out_index, slot_index, group_slots):
    pair_count, rows, width = three_center.shape
    tile = coefficients.shape[1]
    steps = 8 if pair_count % 8 == 0 else 1
    per = pair_count // steps
    zeros = jnp.zeros_like(coefficients)
    w2 = jnp.concatenate(
        [
            jnp.concatenate([coefficients, zeros], axis=2),
            jnp.concatenate([zeros, coefficients], axis=2),
        ],
        axis=1,
    )
    grid_spec = pltpu.PrefetchScalarGridSpec(
        num_scalar_prefetch=2,
        grid=(steps,),
        in_specs=[
            pl.BlockSpec((per, rows, width), lambda i, o, s: (i, 0, 0)),
            pl.BlockSpec((per, 2 * tile, 2 * tile), lambda i, o, s: (i, 0, 0)),
        ],
        out_specs=[pl.BlockSpec(memory_space=pl.ANY)] * len(group_slots),
        scratch_shapes=[
            pltpu.VMEM((2, per, rows, width), three_center.dtype),
            pltpu.SemaphoreType.DMA((2, per)),
        ],
    )
    block_bytes = rows * width * 2
    return pl.pallas_call(
        _transform_kernel,
        grid_spec=grid_spec,
        out_shape=[jax.ShapeDtypeStruct((n, rows, width), three_center.dtype) for n in group_slots],
        compiler_params=pltpu.CompilerParams(dimension_semantics=("arbitrary",)),
        cost_estimate=pl.CostEstimate(
            flops=2 * pair_count * rows * width * 4 * tile,
            transcendentals=0,
            bytes_accessed=2 * pair_count * block_bytes,
        ),
    )(out_index, slot_index, three_center, w2)


def _gram_kernel(lab_ref, x_ref, o_ref, acc, fitted_t):
    step = pl.program_id(0)
    sources, cap = x_ref.shape[0], x_ref.shape[1]
    dom, rows, width = acc.shape
    block = o_ref.shape[0]

    @pl.when(step == 0)
    def _():
        acc[...] = jnp.zeros_like(acc)
        for s in range(sources):
            for c in range(cap):
                e = lab_ref[s * cap + c]

                @pl.when(e >= 0)
                def _():
                    acc[e] += x_ref[s, c].astype(jnp.float32)

        fitted = acc[...].astype(x_ref.dtype).reshape(dom * rows, width)
        fitted_t[...] = fitted.T

    start = pl.multiple_of(step * block, block)
    lhs = acc[pl.ds(pl.multiple_of(step * (block // rows), block // rows), block // rows)]
    lhs = lhs.astype(x_ref.dtype).reshape(block, width)
    o_ref[...] = jnp.dot(lhs, fitted_t[...], preferred_element_type=jnp.float32)


def domain_gram(received, which, labels, dom, row_steps=4):
    sources, slots, rows, width = received.shape
    cap = CAP
    domain_rows = dom * rows
    block = domain_rows // row_steps
    grid_spec = pltpu.PrefetchScalarGridSpec(
        num_scalar_prefetch=1,
        grid=(row_steps,),
        in_specs=[pl.BlockSpec((sources, cap, rows, width), lambda i, lab: (0, which, 0, 0))],
        out_specs=pl.BlockSpec((block, domain_rows), lambda i, lab: (i, 0)),
        scratch_shapes=[
            pltpu.VMEM((dom, rows, width), jnp.float32),
            pltpu.VMEM((width, domain_rows), received.dtype),
        ],
    )
    return pl.pallas_call(
        _gram_kernel,
        grid_spec=grid_spec,
        out_shape=jax.ShapeDtypeStruct((domain_rows, domain_rows), jnp.float32),
        compiler_params=pltpu.CompilerParams(
            dimension_semantics=("arbitrary",), vmem_limit_bytes=60 * 1024 * 1024
        ),
        cost_estimate=pl.CostEstimate(
            flops=2 * domain_rows * domain_rows * width,
            transcendentals=0,
            bytes_accessed=sources * cap * rows * width * 2 + domain_rows * domain_rows * 4,
        ),
    )(labels.reshape(-1), received)


def per_device(three_center, coefficients, target, domain_slot, owner_order):
    pair_count, tile_width, col_width = three_center.shape
    occ_count = lax.axis_size("occ")
    tile_count = owner_order.shape[0]
    owned_tiles = tile_count // occ_count
    slot_count = tile_count * CAP
    tile_ids = jnp.arange(tile_count, dtype=jnp.int32)
    position = jnp.sum(
        jnp.where(owner_order[None, :] == tile_ids[:, None], tile_ids[None, :], 0), axis=1
    )
    pair_ids = jnp.arange(pair_count, dtype=jnp.int32)
    earlier = (target[:, None] == target[None, :]) & (pair_ids[:, None] > pair_ids[None, :])
    rank = jnp.sum(earlier.astype(jnp.int32), axis=1)
    pos = jnp.take(position, target)
    groups = [[0, 1]] + [[k] for k in range(2, owned_tiles)] if owned_tiles > 2 else [[k] for k in range(owned_tiles)]
    group_of = [g for g, group in enumerate(groups) for k in group]
    place_of = [i for group in groups for i, k in enumerate(group)]
    size_of = [len(groups[g]) for g in group_of]
    k_local = pos % owned_tiles
    out_index = jnp.take(jnp.array(group_of, jnp.int32), k_local)
    slot_index = ((pos // owned_tiles) * jnp.take(jnp.array(size_of, jnp.int32), k_local)
                  + jnp.take(jnp.array(place_of, jnp.int32), k_local)) * CAP + rank
    tile_slot = (k_local * occ_count + pos // owned_tiles) * CAP + rank
    labels = jnp.full((slot_count,), -1, jnp.int32).at[tile_slot].set(domain_slot)
    labels = labels.reshape(owned_tiles, occ_count, CAP).transpose(1, 0, 2)
    received_labels = lax.all_to_all(labels, "occ", split_axis=0, concat_axis=0, tiled=True)

    buffers = transform_into_slots(
        three_center, coefficients, out_index, slot_index,
        [occ_count * len(group) * CAP for group in groups],
    )
    pieces = []
    held = ()
    for g, group in enumerate(groups):
        buffer = buffers[g].reshape(occ_count, len(group) * CAP * tile_width, col_width)
        buffer, held = lax.optimization_barrier((buffer, held))
        received = lax.all_to_all(buffer, "occ", split_axis=0, concat_axis=0, tiled=True)
        received = received.reshape(occ_count, len(group) * CAP, tile_width, col_width)
        grams = [domain_gram(received, i, received_labels[:, k], DOM) for i, k in enumerate(group)]
        pieces += [lax.psum_scatter(gm, "aux", scatter_dimension=0, tiled=True) for gm in grams]
        held = tuple(grams)
    return jnp.stack(pieces, axis=1)


def solution(mesh):
    in_specs = (P("occ", None, "aux"), P("occ", None, None), P("occ"), P("occ"), P())
    out_specs = P("aux", "occ", None)
    return jax.shard_map(
        per_device, mesh=mesh, in_specs=in_specs, out_specs=out_specs, check_vma=False
    )
```

```python
import functools
import math

import jax
import jax.numpy as jnp
from jax import lax
from jax.experimental import pallas as pl
from jax.experimental.pallas import tpu as pltpu
from jax.sharding import PartitionSpec as P

DOM = 16
CAP = 2
LANES = 256


def _transform_kernel(out_ref, slot_ref, tc_ref, w_ref, *rest):
    chunks = len(rest) - 2
    outs, (buf, sems) = rest[:chunks], rest[chunks:]
    step = pl.program_id(0)
    steps = pl.num_programs(0)
    per = tc_ref.shape[0]
    rows, width = tc_ref.shape[1], tc_ref.shape[2]
    groups = width // LANES
    half = w_ref.shape[1]
    side = buf.at[step % 2]

    def each_copy(at, parity, act):
        held = buf.at[parity]
        for j in range(per):
            chunk, local = out_ref[at * per + j], slot_ref[at * per + j]
            for kk in range(chunks):
                @pl.when(chunk == kk)
                def _():
                    act(pltpu.make_async_copy(held.at[j], outs[kk].at[local], sems.at[parity, j]))

    def start(cp):
        cp.start()

    def wait(cp):
        cp.wait()

    @pl.when(step >= 2)
    def _():
        each_copy(step - 2, step % 2, wait)

    pad = jnp.zeros((half, half), w_ref.dtype)
    for j in range(per):
        w2 = w_ref[j]
        w4 = jnp.concatenate(
            [jnp.concatenate([w2, pad], axis=1), jnp.concatenate([pad, w2], axis=1)], axis=0
        )
        x = tc_ref[j]
        stacked = jnp.concatenate([x[:, g * LANES:(g + 1) * LANES] for g in range(groups)], axis=0)
        y = jnp.dot(stacked, w4, preferred_element_type=jnp.float32).astype(buf.dtype)
        for g in range(groups):
            side[j, :, g * LANES:(g + 1) * LANES] = y[g * rows:(g + 1) * rows]

    each_copy(step, step % 2, start)

    @pl.when(step == steps - 1)
    def _():
        each_copy(step - 1, (step + 1) % 2, wait)
        each_copy(step, step % 2, wait)


def transform_into_slots(three_center, coefficients, out_index, slot_index, group_slots):
    pair_count, rows, width = three_center.shape
    tile = coefficients.shape[1]
    steps = 8 if pair_count % 8 == 0 else 1
    per = pair_count // steps
    zeros = jnp.zeros_like(coefficients)
    w2 = jnp.concatenate(
        [
            jnp.concatenate([coefficients, zeros], axis=2),
            jnp.concatenate([zeros, coefficients], axis=2),
        ],
        axis=1,
    )
    grid_spec = pltpu.PrefetchScalarGridSpec(
        num_scalar_prefetch=2,
        grid=(steps,),
        in_specs=[
            pl.BlockSpec((per, rows, width), lambda i, o, s: (i, 0, 0)),
            pl.BlockSpec((per, 2 * tile, 2 * tile), lambda i, o, s: (i, 0, 0)),
        ],
        out_specs=[pl.BlockSpec(memory_space=pl.ANY)] * len(group_slots),
        scratch_shapes=[
            pltpu.VMEM((2, per, rows, width), three_center.dtype),
            pltpu.SemaphoreType.DMA((2, per)),
        ],
    )
    block_bytes = rows * width * 2
    return pl.pallas_call(
        _transform_kernel,
        grid_spec=grid_spec,
        out_shape=[jax.ShapeDtypeStruct((n, rows, width), three_center.dtype) for n in group_slots],
        compiler_params=pltpu.CompilerParams(dimension_semantics=("arbitrary",)),
        cost_estimate=pl.CostEstimate(
            flops=2 * pair_count * rows * width * 4 * tile,
            transcendentals=0,
            bytes_accessed=2 * pair_count * block_bytes,
        ),
    )(out_index, slot_index, three_center, w2)


def _gram_kernel(lab_ref, x_ref, o_ref, acc, fs, ft2, *, row_blk):
    sources, cap = x_ref.shape[0], x_ref.shape[1]
    dom, rows, width = acc.shape
    n = dom * rows
    cols = o_ref.shape[1]
    wrap = ft2.shape[1] - n
    acc[...] = jnp.zeros_like(acc)
    for s in range(sources):
        for c in range(cap):
            e = lab_ref[s * cap + c]

            @pl.when(e >= 0)
            def _():
                acc[e] += x_ref[s, c].astype(jnp.float32)

    fs[...] = acc[...].astype(fs.dtype).reshape(n, width)
    ft = fs[...].T
    ft2[:, :n] = ft
    ft2[:, n:] = ft[:, :wrap]
    for a in range(n // row_blk):
        lhs = fs[a * row_blk:(a + 1) * row_blk, :]
        o_ref[a * row_blk:(a + 1) * row_blk, :] = jnp.dot(
            lhs, ft2[:, a * row_blk:a * row_blk + cols], preferred_element_type=jnp.float32
        )


def packed_gram(received, labels, dom, parts):
    sources, cap, rows, width = received.shape
    n = dom * rows
    row_blk = n // parts
    keep = parts // 2 + 1
    cols = keep * row_blk
    grid_spec = pltpu.PrefetchScalarGridSpec(
        num_scalar_prefetch=1,
        grid=(1,),
        in_specs=[pl.BlockSpec((sources, cap, rows, width), lambda i, lab: (0, 0, 0, 0))],
        out_specs=pl.BlockSpec((n, cols), lambda i, lab: (0, 0)),
        scratch_shapes=[
            pltpu.VMEM((dom, rows, width), jnp.float32),
            pltpu.VMEM((n, width), received.dtype),
            pltpu.VMEM((width, n + cols - row_blk), received.dtype),
        ],
    )
    return pl.pallas_call(
        functools.partial(_gram_kernel, row_blk=row_blk),
        grid_spec=grid_spec,
        out_shape=jax.ShapeDtypeStruct((n, cols), jnp.float32),
        compiler_params=pltpu.CompilerParams(
            dimension_semantics=("arbitrary",), vmem_limit_bytes=60 * 1024 * 1024
        ),
        cost_estimate=pl.CostEstimate(
            flops=2 * n * cols * width,
            transcendentals=0,
            bytes_accessed=sources * cap * rows * width * 2 + n * cols * 4,
        ),
    )(labels.reshape(-1), received)


def unpack_rows(reduced, parts):
    rows, cols = reduced.shape
    blk = rows
    keep = cols // blk
    blocks = [reduced[:, j * blk:(j + 1) * blk] for j in range(keep)]
    for p in range(keep, parts):
        shift = parts - p
        sent = reduced[:, shift * blk:(shift + 1) * blk]
        got = lax.ppermute(sent, "aux", perm=[(i, (i + shift) % parts) for i in range(parts)])
        blocks.append(got.T)
    rotated = jnp.concatenate(blocks, axis=1)
    return jnp.roll(rotated, lax.axis_index("aux") * blk, axis=1)


def per_device(three_center, coefficients, target, domain_slot, owner_order):
    pair_count, tile_width, col_width = three_center.shape
    occ_count = lax.axis_size("occ")
    aux_count = lax.axis_size("aux")
    tile_count = owner_order.shape[0]
    owned_tiles = tile_count // occ_count
    slot_count = tile_count * CAP
    tile_ids = jnp.arange(tile_count, dtype=jnp.int32)
    position = jnp.sum(
        jnp.where(owner_order[None, :] == tile_ids[:, None], tile_ids[None, :], 0), axis=1
    )
    pair_ids = jnp.arange(pair_count, dtype=jnp.int32)
    earlier = (target[:, None] == target[None, :]) & (pair_ids[:, None] > pair_ids[None, :])
    rank = jnp.sum(earlier.astype(jnp.int32), axis=1)
    pos = jnp.take(position, target)
    out_index = pos % owned_tiles
    slot_index = (pos // owned_tiles) * CAP + rank
    labels = jnp.full((slot_count,), -1, jnp.int32).at[out_index * occ_count * CAP + slot_index].set(domain_slot)
    labels = labels.reshape(owned_tiles, occ_count, CAP).transpose(1, 0, 2)
    received_labels = lax.all_to_all(labels, "occ", split_axis=0, concat_axis=0, tiled=True)

    buffers = transform_into_slots(
        three_center, coefficients, out_index, slot_index, [occ_count * CAP] * owned_tiles
    )
    pieces = []
    for k in range(owned_tiles):
        buffer = buffers[k].reshape(occ_count, CAP * tile_width, col_width)
        received = lax.all_to_all(buffer, "occ", split_axis=0, concat_axis=0, tiled=True)
        received = received.reshape(occ_count, CAP, tile_width, col_width)
        packed = packed_gram(received, received_labels[:, k], DOM, aux_count)
        reduced = lax.psum_scatter(packed, "aux", scatter_dimension=0, tiled=True)
        pieces.append(unpack_rows(reduced, aux_count))
    return jnp.stack(pieces, axis=1)


def solution(mesh):
    in_specs = (P("occ", None, "aux"), P("occ", None, None), P("occ"), P("occ"), P())
    out_specs = P("aux", "occ", None)
    return jax.shard_map(
        per_device, mesh=mesh, in_specs=in_specs, out_specs=out_specs, check_vma=False
    )
```

```python
import functools
import math

import jax
import jax.numpy as jnp
from jax import lax
from jax.experimental import pallas as pl
from jax.experimental.pallas import tpu as pltpu
from jax.sharding import PartitionSpec as P

DOM = 16
CAP = 2
LANES = 256


def _transform_kernel(out_ref, slot_ref, tc_ref, w_ref, *rest):
    chunks = len(rest) - 2
    outs, (buf, sems) = rest[:chunks], rest[chunks:]
    step = pl.program_id(0)
    steps = pl.num_programs(0)
    per = tc_ref.shape[0]
    rows, width = tc_ref.shape[1], tc_ref.shape[2]
    groups = width // LANES
    half = w_ref.shape[1]
    side = buf.at[step % 2]

    def each_copy(at, parity, act):
        held = buf.at[parity]
        for j in range(per):
            chunk, local = out_ref[at * per + j], slot_ref[at * per + j]
            for kk in range(chunks):
                @pl.when(chunk == kk)
                def _():
                    act(pltpu.make_async_copy(held.at[j], outs[kk].at[local], sems.at[parity, j]))

    def start(cp):
        cp.start()

    def wait(cp):
        cp.wait()

    @pl.when(step >= 2)
    def _():
        each_copy(step - 2, step % 2, wait)

    pad = jnp.zeros((half, half), w_ref.dtype)
    for j in range(per):
        w2 = w_ref[j]
        w4 = jnp.concatenate(
            [jnp.concatenate([w2, pad], axis=1), jnp.concatenate([pad, w2], axis=1)], axis=0
        )
        x = tc_ref[j]
        stacked = jnp.concatenate([x[:, g * LANES:(g + 1) * LANES] for g in range(groups)], axis=0)
        y = jnp.dot(stacked, w4, preferred_element_type=jnp.float32).astype(buf.dtype)
        for g in range(groups):
            side[j, :, g * LANES:(g + 1) * LANES] = y[g * rows:(g + 1) * rows]

    each_copy(step, step % 2, start)

    @pl.when(step == steps - 1)
    def _():
        each_copy(step - 1, (step + 1) % 2, wait)
        each_copy(step, step % 2, wait)


def transform_into_slots(three_center, coefficients, out_index, slot_index, group_slots):
    pair_count, rows, width = three_center.shape
    tile = coefficients.shape[1]
    steps = 8 if pair_count % 8 == 0 else 1
    per = pair_count // steps
    zeros = jnp.zeros_like(coefficients)
    w2 = jnp.concatenate(
        [
            jnp.concatenate([coefficients, zeros], axis=2),
            jnp.concatenate([zeros, coefficients], axis=2),
        ],
        axis=1,
    )
    grid_spec = pltpu.PrefetchScalarGridSpec(
        num_scalar_prefetch=2,
        grid=(steps,),
        in_specs=[
            pl.BlockSpec((per, rows, width), lambda i, o, s: (i, 0, 0)),
            pl.BlockSpec((per, 2 * tile, 2 * tile), lambda i, o, s: (i, 0, 0)),
        ],
        out_specs=[pl.BlockSpec(memory_space=pl.ANY)] * len(group_slots),
        scratch_shapes=[
            pltpu.VMEM((2, per, rows, width), three_center.dtype),
            pltpu.SemaphoreType.DMA((2, per)),
        ],
    )
    block_bytes = rows * width * 2
    return pl.pallas_call(
        _transform_kernel,
        grid_spec=grid_spec,
        out_shape=[jax.ShapeDtypeStruct((n, rows, width), three_center.dtype) for n in group_slots],
        compiler_params=pltpu.CompilerParams(dimension_semantics=("arbitrary",)),
        cost_estimate=pl.CostEstimate(
            flops=2 * pair_count * rows * width * 4 * tile,
            transcendentals=0,
            bytes_accessed=2 * pair_count * block_bytes,
        ),
    )(out_index, slot_index, three_center, w2)


def _gram_kernel(lab_ref, x_ref, o_ref, acc, fs, ft2, *, row_blk):
    sources, cap = x_ref.shape[0], x_ref.shape[1]
    dom, rows, width = acc.shape
    n = dom * rows
    cols = o_ref.shape[1]
    wrap = ft2.shape[1] - n
    acc[...] = jnp.zeros_like(acc)
    for s in range(sources):
        for c in range(cap):
            e = lab_ref[s * cap + c]

            @pl.when(e >= 0)
            def _():
                acc[e] += x_ref[s, c].astype(jnp.float32)

    fs[...] = acc[...].astype(fs.dtype).reshape(n, width)
    ft = fs[...].T
    ft2[:, :n] = ft
    ft2[:, n:] = ft[:, :wrap]
    for a in range(n // row_blk):
        lhs = fs[a * row_blk:(a + 1) * row_blk, :]
        o_ref[a * row_blk:(a + 1) * row_blk, :] = jnp.dot(
            lhs, ft2[:, a * row_blk:a * row_blk + cols], preferred_element_type=jnp.float32
        )


def packed_gram(received, labels, dom, parts):
    sources, cap, rows, width = received.shape
    n = dom * rows
    row_blk = n // parts
    keep = parts // 2 + 1
    cols = keep * row_blk
    grid_spec = pltpu.PrefetchScalarGridSpec(
        num_scalar_prefetch=1,
        grid=(1,),
        in_specs=[pl.BlockSpec((sources, cap, rows, width), lambda i, lab: (0, 0, 0, 0))],
        out_specs=pl.BlockSpec((n, cols), lambda i, lab: (0, 0)),
        scratch_shapes=[
            pltpu.VMEM((dom, rows, width), jnp.float32),
            pltpu.VMEM((n, width), received.dtype),
            pltpu.VMEM((width, n + cols - row_blk), received.dtype),
        ],
    )
    return pl.pallas_call(
        functools.partial(_gram_kernel, row_blk=row_blk),
        grid_spec=grid_spec,
        out_shape=jax.ShapeDtypeStruct((n, cols), jnp.float32),
        compiler_params=pltpu.CompilerParams(
            dimension_semantics=("arbitrary",), vmem_limit_bytes=60 * 1024 * 1024
        ),
        cost_estimate=pl.CostEstimate(
            flops=2 * n * cols * width,
            transcendentals=0,
            bytes_accessed=sources * cap * rows * width * 2 + n * cols * 4,
        ),
    )(labels.reshape(-1), received)


def unpack_rows(reduced, parts):
    rows, cols = reduced.shape
    blk = rows
    keep = cols // blk
    blocks = [reduced[:, j * blk:(j + 1) * blk] for j in range(keep)]
    for p in range(keep, parts):
        shift = parts - p
        sent = reduced[:, shift * blk:(shift + 1) * blk]
        got = lax.ppermute(sent, "aux", perm=[(i, (i + shift) % parts) for i in range(parts)])
        blocks.append(got.T)
    rotated = jnp.concatenate(blocks, axis=1)
    return jnp.roll(rotated, lax.axis_index("aux") * blk, axis=1)


def per_device(three_center, coefficients, target, domain_slot, owner_order):
    pair_count, tile_width, col_width = three_center.shape
    occ_count = lax.axis_size("occ")
    aux_count = lax.axis_size("aux")
    tile_count = owner_order.shape[0]
    owned_tiles = tile_count // occ_count
    slot_count = tile_count * CAP
    tile_ids = jnp.arange(tile_count, dtype=jnp.int32)
    position = jnp.sum(
        jnp.where(owner_order[None, :] == tile_ids[:, None], tile_ids[None, :], 0), axis=1
    )
    pair_ids = jnp.arange(pair_count, dtype=jnp.int32)
    earlier = (target[:, None] == target[None, :]) & (pair_ids[:, None] > pair_ids[None, :])
    rank = jnp.sum(earlier.astype(jnp.int32), axis=1)
    pos = jnp.take(position, target)
    out_index = pos % owned_tiles
    slot_index = (pos // owned_tiles) * CAP + rank
    labels = jnp.full((slot_count,), -1, jnp.int32).at[out_index * occ_count * CAP + slot_index].set(domain_slot)
    labels = labels.reshape(owned_tiles, occ_count, CAP).transpose(1, 0, 2)
    received_labels = lax.all_to_all(labels, "occ", split_axis=0, concat_axis=0, tiled=True)

    buffers = transform_into_slots(
        three_center, coefficients, out_index, slot_index, [occ_count * CAP] * owned_tiles
    )
    pieces = []
    for k in range(owned_tiles):
        buffer = buffers[k].reshape(occ_count, CAP * tile_width, col_width)
        if k == 2:
            buffer, pieces[0] = lax.optimization_barrier((buffer, pieces[0]))
        received = lax.all_to_all(buffer, "occ", split_axis=0, concat_axis=0, tiled=True)
        if k == 3:
            received, pieces[1] = lax.optimization_barrier((received, pieces[1]))
        received = received.reshape(occ_count, CAP, tile_width, col_width)
        packed = packed_gram(received, received_labels[:, k], DOM, aux_count)
        reduced = lax.psum_scatter(packed, "aux", scatter_dimension=0, tiled=True)
        pieces.append(unpack_rows(reduced, aux_count))
    return jnp.stack(pieces, axis=1)


def solution(mesh):
    in_specs = (P("occ", None, "aux"), P("occ", None, None), P("occ"), P("occ"), P())
    out_specs = P("aux", "occ", None)
    return jax.shard_map(
        per_device, mesh=mesh, in_specs=in_specs, out_specs=out_specs, check_vma=False
    )
```

```python
import math

import jax
import jax.numpy as jnp
from jax import lax
from jax.experimental import pallas as pl
from jax.experimental.pallas import tpu as pltpu
from jax.sharding import PartitionSpec as P

DOM = 16
CAP = 2
LANES = 256


def _transform_kernel(out_ref, slot_ref, tc_ref, w_ref, *rest):
    chunks = len(rest) - 2
    outs, (buf, sems) = rest[:chunks], rest[chunks:]
    step = pl.program_id(0)
    steps = pl.num_programs(0)
    per = tc_ref.shape[0]
    rows, width = tc_ref.shape[1], tc_ref.shape[2]
    groups = width // LANES
    half = w_ref.shape[1]
    side = buf.at[step % 2]

    def each_copy(at, parity, act):
        held = buf.at[parity]
        for j in range(per):
            chunk, local = out_ref[at * per + j], slot_ref[at * per + j]
            for kk in range(chunks):
                @pl.when(chunk == kk)
                def _():
                    act(pltpu.make_async_copy(held.at[j], outs[kk].at[local], sems.at[parity, j]))

    def start(cp):
        cp.start()

    def wait(cp):
        cp.wait()

    @pl.when(step >= 2)
    def _():
        each_copy(step - 2, step % 2, wait)

    pad = jnp.zeros((half, half), w_ref.dtype)
    for j in range(per):
        w2 = w_ref[j]
        w4 = jnp.concatenate(
            [jnp.concatenate([w2, pad], axis=1), jnp.concatenate([pad, w2], axis=1)], axis=0
        )
        x = tc_ref[j]
        stacked = jnp.concatenate([x[:, g * LANES:(g + 1) * LANES] for g in range(groups)], axis=0)
        y = jnp.dot(stacked, w4, preferred_element_type=jnp.float32).astype(buf.dtype)
        for g in range(groups):
            side[j, :, g * LANES:(g + 1) * LANES] = y[g * rows:(g + 1) * rows]

    each_copy(step, step % 2, start)

    @pl.when(step == steps - 1)
    def _():
        each_copy(step - 1, (step + 1) % 2, wait)
        each_copy(step, step % 2, wait)


def transform_into_slots(three_center, coefficients, out_index, slot_index, group_slots):
    pair_count, rows, width = three_center.shape
    tile = coefficients.shape[1]
    steps = 8 if pair_count % 8 == 0 else 1
    per = pair_count // steps
    zeros = jnp.zeros_like(coefficients)
    w2 = jnp.concatenate(
        [
            jnp.concatenate([coefficients, zeros], axis=2),
            jnp.concatenate([zeros, coefficients], axis=2),
        ],
        axis=1,
    )
    grid_spec = pltpu.PrefetchScalarGridSpec(
        num_scalar_prefetch=2,
        grid=(steps,),
        in_specs=[
            pl.BlockSpec((per, rows, width), lambda i, o, s: (i, 0, 0)),
            pl.BlockSpec((per, 2 * tile, 2 * tile), lambda i, o, s: (i, 0, 0)),
        ],
        out_specs=[pl.BlockSpec(memory_space=pl.ANY)] * len(group_slots),
        scratch_shapes=[
            pltpu.VMEM((2, per, rows, width), three_center.dtype),
            pltpu.SemaphoreType.DMA((2, per)),
        ],
    )
    block_bytes = rows * width * 2
    return pl.pallas_call(
        _transform_kernel,
        grid_spec=grid_spec,
        out_shape=[jax.ShapeDtypeStruct((n, rows, width), three_center.dtype) for n in group_slots],
        compiler_params=pltpu.CompilerParams(dimension_semantics=("arbitrary",)),
        cost_estimate=pl.CostEstimate(
            flops=2 * pair_count * rows * width * 4 * tile,
            transcendentals=0,
            bytes_accessed=2 * pair_count * block_bytes,
        ),
    )(out_index, slot_index, three_center, w2)


def _gram_kernel(lab_ref, x_ref, o_ref, acc):
    k = pl.program_id(0)
    sources, cap = x_ref.shape[0], x_ref.shape[1]
    per_source = lab_ref.shape[0] // sources
    acc[...] = jnp.zeros_like(acc)
    for s in range(sources):
        for c in range(cap):
            e = lab_ref[s * per_source + k * cap + c]

            @pl.when(e >= 0)
            def _():
                acc[e] += x_ref[s, c].astype(jnp.float32)

    dom, rows, width = acc.shape
    fitted = acc[...].astype(x_ref.dtype).reshape(dom * rows, width)
    o_ref[...] = lax.dot_general(
        fitted, fitted, (((1,), (1,)), ((), ())), preferred_element_type=jnp.float32
    )


def domain_gram(received, labels, dom):
    sources, slots, rows, width = received.shape
    owned = slots // CAP
    domain_rows = dom * rows
    grid_spec = pltpu.PrefetchScalarGridSpec(
        num_scalar_prefetch=1,
        grid=(owned,),
        in_specs=[pl.BlockSpec((sources, CAP, rows, width), lambda k, lab: (0, k, 0, 0))],
        out_specs=pl.BlockSpec((domain_rows, domain_rows), lambda k, lab: (0, k)),
        scratch_shapes=[pltpu.VMEM((dom, rows, width), jnp.float32)],
    )
    return pl.pallas_call(
        _gram_kernel,
        grid_spec=grid_spec,
        out_shape=jax.ShapeDtypeStruct((domain_rows, owned * domain_rows), jnp.float32),
        compiler_params=pltpu.CompilerParams(
            dimension_semantics=("arbitrary",), vmem_limit_bytes=60 * 1024 * 1024
        ),
        cost_estimate=pl.CostEstimate(
            flops=2 * owned * domain_rows * domain_rows * width,
            transcendentals=0,
            bytes_accessed=sources * slots * rows * width * 2 + owned * domain_rows * domain_rows * 4,
        ),
    )(labels.reshape(-1), received)


def per_device(three_center, coefficients, target, domain_slot, owner_order):
    pair_count, tile_width, col_width = three_center.shape
    occ_count = lax.axis_size("occ")
    aux_count = lax.axis_size("aux")
    tile_count = owner_order.shape[0]
    owned_tiles = tile_count // occ_count
    slot_count = tile_count * CAP
    tile_ids = jnp.arange(tile_count, dtype=jnp.int32)
    position = jnp.sum(
        jnp.where(owner_order[None, :] == tile_ids[:, None], tile_ids[None, :], 0), axis=1
    )
    pair_ids = jnp.arange(pair_count, dtype=jnp.int32)
    earlier = (target[:, None] == target[None, :]) & (pair_ids[:, None] > pair_ids[None, :])
    rank = jnp.sum(earlier.astype(jnp.int32), axis=1)
    pos = jnp.take(position, target)
    out_index = pos % owned_tiles
    slot_index = (pos // owned_tiles) * CAP + rank
    labels = jnp.full((slot_count,), -1, jnp.int32).at[out_index * occ_count * CAP + slot_index].set(domain_slot)
    labels = labels.reshape(owned_tiles, occ_count, CAP).transpose(1, 0, 2)
    received_labels = lax.all_to_all(labels, "occ", split_axis=0, concat_axis=0, tiled=True)

    buffers = transform_into_slots(
        three_center, coefficients, out_index, slot_index, [occ_count * CAP] * owned_tiles
    )
    pieces = []
    for k in range(owned_tiles):
        buffer = buffers[k].reshape(occ_count, CAP * tile_width, col_width)
        received = lax.all_to_all(buffer, "occ", split_axis=0, concat_axis=0, tiled=True)
        received = received.reshape(occ_count, CAP, tile_width, col_width)
        partial_gram = domain_gram(received, received_labels[:, k], DOM)
        pieces.append(lax.psum_scatter(partial_gram, "aux", scatter_dimension=0, tiled=True))
    return jnp.stack(pieces, axis=1)


def solution(mesh):
    in_specs = (P("occ", None, "aux"), P("occ", None, None), P("occ"), P("occ"), P())
    out_specs = P("aux", "occ", None)
    return jax.shard_map(
        per_device, mesh=mesh, in_specs=in_specs, out_specs=out_specs, check_vma=False
    )
```

```python
import math

import jax
import jax.numpy as jnp
from jax import lax
from jax.experimental import pallas as pl
from jax.experimental.pallas import tpu as pltpu
from jax.sharding import PartitionSpec as P

DOM = 16
CAP = 2
LANES = 256


def _transform_kernel(out_ref, slot_ref, tc_ref, w_ref, *rest):
    chunks = len(rest) - 2
    outs, (buf, sems) = rest[:chunks], rest[chunks:]
    step = pl.program_id(0)
    steps = pl.num_programs(0)
    per = tc_ref.shape[0]
    rows, width = tc_ref.shape[1], tc_ref.shape[2]
    groups = width // LANES
    half = w_ref.shape[1]
    side = buf.at[step % 2]

    def each_copy(at, parity, act):
        held = buf.at[parity]
        for j in range(per):
            chunk, local = out_ref[at * per + j], slot_ref[at * per + j]
            for kk in range(chunks):
                @pl.when(chunk == kk)
                def _():
                    act(pltpu.make_async_copy(held.at[j], outs[kk].at[local], sems.at[parity, j]))

    def start(cp):
        cp.start()

    def wait(cp):
        cp.wait()

    @pl.when(step >= 2)
    def _():
        each_copy(step - 2, step % 2, wait)

    pad = jnp.zeros((half, half), w_ref.dtype)
    for j in range(per):
        w2 = w_ref[j]
        w4 = jnp.concatenate(
            [jnp.concatenate([w2, pad], axis=1), jnp.concatenate([pad, w2], axis=1)], axis=0
        )
        x = tc_ref[j]
        stacked = jnp.concatenate([x[:, g * LANES:(g + 1) * LANES] for g in range(groups)], axis=0)
        y = jnp.dot(stacked, w4, preferred_element_type=jnp.float32).astype(buf.dtype)
        for g in range(groups):
            side[j, :, g * LANES:(g + 1) * LANES] = y[g * rows:(g + 1) * rows]

    each_copy(step, step % 2, start)

    @pl.when(step == steps - 1)
    def _():
        each_copy(step - 1, (step + 1) % 2, wait)
        each_copy(step, step % 2, wait)


def transform_into_slots(three_center, coefficients, out_index, slot_index, group_slots):
    pair_count, rows, width = three_center.shape
    tile = coefficients.shape[1]
    steps = 8 if pair_count % 8 == 0 else 1
    per = pair_count // steps
    zeros = jnp.zeros_like(coefficients)
    w2 = jnp.concatenate(
        [
            jnp.concatenate([coefficients, zeros], axis=2),
            jnp.concatenate([zeros, coefficients], axis=2),
        ],
        axis=1,
    )
    grid_spec = pltpu.PrefetchScalarGridSpec(
        num_scalar_prefetch=2,
        grid=(steps,),
        in_specs=[
            pl.BlockSpec((per, rows, width), lambda i, o, s: (i, 0, 0)),
            pl.BlockSpec((per, 2 * tile, 2 * tile), lambda i, o, s: (i, 0, 0)),
        ],
        out_specs=[pl.BlockSpec(memory_space=pl.ANY)] * len(group_slots),
        scratch_shapes=[
            pltpu.VMEM((2, per, rows, width), three_center.dtype),
            pltpu.SemaphoreType.DMA((2, per)),
        ],
    )
    block_bytes = rows * width * 2
    return pl.pallas_call(
        _transform_kernel,
        grid_spec=grid_spec,
        out_shape=[jax.ShapeDtypeStruct((n, rows, width), three_center.dtype) for n in group_slots],
        compiler_params=pltpu.CompilerParams(dimension_semantics=("arbitrary",)),
        cost_estimate=pl.CostEstimate(
            flops=2 * pair_count * rows * width * 4 * tile,
            transcendentals=0,
            bytes_accessed=2 * pair_count * block_bytes,
        ),
    )(out_index, slot_index, three_center, w2)


def _gram_kernel(lab_ref, *refs):
    x_refs, (o_ref, acc) = refs[:-2], refs[-2:]
    cap = len(x_refs)
    sources = x_refs[0].shape[0]
    acc[...] = jnp.zeros_like(acc)
    for s in range(sources):
        for c in range(cap):
            e = lab_ref[s * cap + c]

            @pl.when(e >= 0)
            def _():
                acc[e] += x_refs[c][s].astype(jnp.float32)

    dom, rows, width = acc.shape
    fitted = acc[...].astype(x_refs[0].dtype).reshape(dom * rows, width)
    o_ref[...] = lax.dot_general(
        fitted, fitted, (((1,), (1,)), ((), ())), preferred_element_type=jnp.float32
    )


def domain_gram(received, labels, dom):
    sources, rows, width = received[0].shape
    cap = len(received)
    domain_rows = dom * rows
    grid_spec = pltpu.PrefetchScalarGridSpec(
        num_scalar_prefetch=1,
        grid=(1,),
        in_specs=[pl.BlockSpec((sources, rows, width), lambda k, lab: (0, 0, 0))] * cap,
        out_specs=pl.BlockSpec((domain_rows, domain_rows), lambda k, lab: (0, 0)),
        scratch_shapes=[pltpu.VMEM((dom, rows, width), jnp.float32)],
    )
    return pl.pallas_call(
        _gram_kernel,
        grid_spec=grid_spec,
        out_shape=jax.ShapeDtypeStruct((domain_rows, domain_rows), jnp.float32),
        compiler_params=pltpu.CompilerParams(
            dimension_semantics=("arbitrary",), vmem_limit_bytes=60 * 1024 * 1024
        ),
        cost_estimate=pl.CostEstimate(
            flops=2 * domain_rows * domain_rows * width,
            transcendentals=0,
            bytes_accessed=cap * sources * rows * width * 2 + domain_rows * domain_rows * 4,
        ),
    )(labels.reshape(-1), *received)


def per_device(three_center, coefficients, target, domain_slot, owner_order):
    pair_count, tile_width, col_width = three_center.shape
    occ_count = lax.axis_size("occ")
    aux_count = lax.axis_size("aux")
    tile_count = owner_order.shape[0]
    owned_tiles = tile_count // occ_count
    slot_count = tile_count * CAP
    tile_ids = jnp.arange(tile_count, dtype=jnp.int32)
    position = jnp.sum(
        jnp.where(owner_order[None, :] == tile_ids[:, None], tile_ids[None, :], 0), axis=1
    )
    pair_ids = jnp.arange(pair_count, dtype=jnp.int32)
    earlier = (target[:, None] == target[None, :]) & (pair_ids[:, None] > pair_ids[None, :])
    rank = jnp.sum(earlier.astype(jnp.int32), axis=1)
    pos = jnp.take(position, target)
    out_index = (pos % owned_tiles) * CAP + rank
    slot_index = pos // owned_tiles
    labels = jnp.full((slot_count,), -1, jnp.int32).at[((pos % owned_tiles) * occ_count + slot_index) * CAP + rank].set(domain_slot)
    labels = labels.reshape(owned_tiles, occ_count, CAP).transpose(1, 0, 2)
    received_labels = lax.all_to_all(labels, "occ", split_axis=0, concat_axis=0, tiled=True)

    buffers = transform_into_slots(
        three_center, coefficients, out_index, slot_index, [occ_count] * (owned_tiles * CAP)
    )
    pieces = []
    for k in range(owned_tiles):
        received = [
            lax.all_to_all(buffers[k * CAP + c], "occ", split_axis=0, concat_axis=0, tiled=True)
            for c in range(CAP)
        ]
        partial_gram = domain_gram(received, received_labels[:, k], DOM)
        pieces.append(lax.psum_scatter(partial_gram, "aux", scatter_dimension=0, tiled=True))
    return jnp.stack(pieces, axis=1)


def solution(mesh):
    in_specs = (P("occ", None, "aux"), P("occ", None, None), P("occ"), P("occ"), P())
    out_specs = P("aux", "occ", None)
    return jax.shard_map(
        per_device, mesh=mesh, in_specs=in_specs, out_specs=out_specs, check_vma=False
    )
```

```python
import math

import jax
import jax.numpy as jnp
from jax import lax
from jax.experimental import pallas as pl
from jax.experimental.pallas import tpu as pltpu
from jax.sharding import PartitionSpec as P

DOM = 16
CAP = 2
LANES = 256


def _transform_kernel(out_ref, slot_ref, tc_ref, w_ref, *rest):
    chunks = len(rest) - 2
    outs, (buf, sems) = rest[:chunks], rest[chunks:]
    step = pl.program_id(0)
    steps = pl.num_programs(0)
    per = tc_ref.shape[0]
    rows, width = tc_ref.shape[1], tc_ref.shape[2]
    groups = width // LANES
    half = w_ref.shape[1]
    side = buf.at[step % 2]

    def each_copy(at, parity, act):
        held = buf.at[parity]
        for j in range(per):
            chunk, local = out_ref[at * per + j], slot_ref[at * per + j]
            for kk in range(chunks):
                @pl.when(chunk == kk)
                def _():
                    act(pltpu.make_async_copy(held.at[j], outs[kk].at[local], sems.at[parity, j]))

    def start(cp):
        cp.start()

    def wait(cp):
        cp.wait()

    @pl.when(step >= 2)
    def _():
        each_copy(step - 2, step % 2, wait)

    pad = jnp.zeros((half, half), w_ref.dtype)
    for j in range(per):
        w2 = w_ref[j]
        w4 = jnp.concatenate(
            [jnp.concatenate([w2, pad], axis=1), jnp.concatenate([pad, w2], axis=1)], axis=0
        )
        x = tc_ref[j]
        stacked = jnp.concatenate([x[:, g * LANES:(g + 1) * LANES] for g in range(groups)], axis=0)
        y = jnp.dot(stacked, w4, preferred_element_type=jnp.float32).astype(buf.dtype)
        for g in range(groups):
            side[j, :, g * LANES:(g + 1) * LANES] = y[g * rows:(g + 1) * rows]

    each_copy(step, step % 2, start)

    @pl.when(step == steps - 1)
    def _():
        each_copy(step - 1, (step + 1) % 2, wait)
        each_copy(step, step % 2, wait)


def transform_into_slots(three_center, coefficients, out_index, slot_index, group_slots):
    pair_count, rows, width = three_center.shape
    tile = coefficients.shape[1]
    steps = 8 if pair_count % 8 == 0 else 1
    per = pair_count // steps
    zeros = jnp.zeros_like(coefficients)
    w2 = jnp.concatenate(
        [
            jnp.concatenate([coefficients, zeros], axis=2),
            jnp.concatenate([zeros, coefficients], axis=2),
        ],
        axis=1,
    )
    grid_spec = pltpu.PrefetchScalarGridSpec(
        num_scalar_prefetch=2,
        grid=(steps,),
        in_specs=[
            pl.BlockSpec((per, rows, width), lambda i, o, s: (i, 0, 0)),
            pl.BlockSpec((per, 2 * tile, 2 * tile), lambda i, o, s: (i, 0, 0)),
        ],
        out_specs=[pl.BlockSpec(memory_space=pl.ANY)] * len(group_slots),
        scratch_shapes=[
            pltpu.VMEM((2, per, rows, width), three_center.dtype),
            pltpu.SemaphoreType.DMA((2, per)),
        ],
    )
    block_bytes = rows * width * 2
    return pl.pallas_call(
        _transform_kernel,
        grid_spec=grid_spec,
        out_shape=[jax.ShapeDtypeStruct((n, rows, width), three_center.dtype) for n in group_slots],
        compiler_params=pltpu.CompilerParams(dimension_semantics=("arbitrary",)),
        cost_estimate=pl.CostEstimate(
            flops=2 * pair_count * rows * width * 4 * tile,
            transcendentals=0,
            bytes_accessed=2 * pair_count * block_bytes,
        ),
    )(out_index, slot_index, three_center, w2)


def _gram_kernel(lab_ref, x_ref, o_ref, acc, fs):
    step = pl.program_id(0)
    half, cap = x_ref.shape[0], x_ref.shape[1]
    dom, rows, width = acc.shape
    block = o_ref.shape[0]

    @pl.when(step == 0)
    def _():
        acc[...] = jnp.zeros_like(acc)

    def accumulate(part):
        for s in range(half):
            for c in range(cap):
                e = lab_ref[(part * half + s) * cap + c]

                @pl.when(e >= 0)
                def _():
                    acc[e] += x_ref[s, c].astype(jnp.float32)

    @pl.when(step == 0)
    def _():
        accumulate(0)

    @pl.when(step == 1)
    def _():
        accumulate(1)
        fs[...] = acc[...].astype(fs.dtype).reshape(dom * rows, width)

    for part in range(2):
        @pl.when(step == part + 1)
        def _():
            lhs = fs[part * block:(part + 1) * block, :]
            o_ref[...] = lax.dot_general(
                lhs, fs[...], (((1,), (1,)), ((), ())), preferred_element_type=jnp.float32
            )


def domain_gram(received, labels, dom):
    sources, slots, rows, width = received.shape
    domain_rows = dom * rows
    half = sources // 2
    grid_spec = pltpu.PrefetchScalarGridSpec(
        num_scalar_prefetch=1,
        grid=(3,),
        in_specs=[pl.BlockSpec((half, CAP, rows, width), lambda i, lab: (jnp.minimum(i, 1), 0, 0, 0))],
        out_specs=pl.BlockSpec((domain_rows // 2, domain_rows), lambda i, lab: (jnp.maximum(i - 1, 0), 0)),
        scratch_shapes=[
            pltpu.VMEM((dom, rows, width), jnp.float32),
            pltpu.VMEM((domain_rows, width), received.dtype),
        ],
    )
    return pl.pallas_call(
        _gram_kernel,
        grid_spec=grid_spec,
        out_shape=jax.ShapeDtypeStruct((domain_rows, domain_rows), jnp.float32),
        compiler_params=pltpu.CompilerParams(
            dimension_semantics=("arbitrary",), vmem_limit_bytes=60 * 1024 * 1024
        ),
        cost_estimate=pl.CostEstimate(
            flops=2 * domain_rows * domain_rows * width,
            transcendentals=0,
            bytes_accessed=sources * slots * rows * width * 2 + domain_rows * domain_rows * 4,
        ),
    )(labels.reshape(-1), received)


def per_device(three_center, coefficients, target, domain_slot, owner_order):
    pair_count, tile_width, col_width = three_center.shape
    occ_count = lax.axis_size("occ")
    aux_count = lax.axis_size("aux")
    tile_count = owner_order.shape[0]
    owned_tiles = tile_count // occ_count
    slot_count = tile_count * CAP
    tile_ids = jnp.arange(tile_count, dtype=jnp.int32)
    position = jnp.sum(
        jnp.where(owner_order[None, :] == tile_ids[:, None], tile_ids[None, :], 0), axis=1
    )
    pair_ids = jnp.arange(pair_count, dtype=jnp.int32)
    earlier = (target[:, None] == target[None, :]) & (pair_ids[:, None] > pair_ids[None, :])
    rank = jnp.sum(earlier.astype(jnp.int32), axis=1)
    pos = jnp.take(position, target)
    out_index = pos % owned_tiles
    slot_index = (pos // owned_tiles) * CAP + rank
    labels = jnp.full((slot_count,), -1, jnp.int32).at[out_index * occ_count * CAP + slot_index].set(domain_slot)
    labels = labels.reshape(owned_tiles, occ_count, CAP).transpose(1, 0, 2)
    received_labels = lax.all_to_all(labels, "occ", split_axis=0, concat_axis=0, tiled=True)

    buffers = transform_into_slots(
        three_center, coefficients, out_index, slot_index, [occ_count * CAP] * owned_tiles
    )
    pieces = []
    for k in range(owned_tiles):
        buffer = buffers[k].reshape(occ_count, CAP * tile_width, col_width)
        received = lax.all_to_all(buffer, "occ", split_axis=0, concat_axis=0, tiled=True)
        received = received.reshape(occ_count, CAP, tile_width, col_width)
        partial_gram = domain_gram(received, received_labels[:, k], DOM)
        pieces.append(lax.psum_scatter(partial_gram, "aux", scatter_dimension=0, tiled=True))
    return jnp.stack(pieces, axis=1)


def solution(mesh):
    in_specs = (P("occ", None, "aux"), P("occ", None, None), P("occ"), P("occ"), P())
    out_specs = P("aux", "occ", None)
    return jax.shard_map(
        per_device, mesh=mesh, in_specs=in_specs, out_specs=out_specs, check_vma=False
    )
```

```python
import math

import jax
import jax.numpy as jnp
from jax import lax
from jax.experimental import pallas as pl
from jax.experimental.pallas import tpu as pltpu
from jax.sharding import PartitionSpec as P

DOM = 16
CAP = 2
LANES = 256


def _transform_kernel(out_ref, slot_ref, tc_ref, w_ref, *rest):
    chunks = len(rest) - 2
    outs, (buf, sems) = rest[:chunks], rest[chunks:]
    step = pl.program_id(0)
    steps = pl.num_programs(0)
    per = tc_ref.shape[0]
    rows, width = tc_ref.shape[1], tc_ref.shape[2]
    groups = width // LANES
    half = w_ref.shape[1]
    side = buf.at[step % 2]

    def each_copy(at, parity, act):
        held = buf.at[parity]
        for j in range(per):
            chunk, local = out_ref[at * per + j], slot_ref[at * per + j]
            for kk in range(chunks):
                @pl.when(chunk == kk)
                def _():
                    act(pltpu.make_async_copy(held.at[j], outs[kk].at[local], sems.at[parity, j]))

    def start(cp):
        cp.start()

    def wait(cp):
        cp.wait()

    @pl.when(step >= 2)
    def _():
        each_copy(step - 2, step % 2, wait)

    pad = jnp.zeros((half, half), w_ref.dtype)
    for j in range(per):
        w2 = w_ref[j]
        w4 = jnp.concatenate(
            [jnp.concatenate([w2, pad], axis=1), jnp.concatenate([pad, w2], axis=1)], axis=0
        )
        x = tc_ref[j]
        stacked = jnp.concatenate([x[:, g * LANES:(g + 1) * LANES] for g in range(groups)], axis=0)
        y = jnp.dot(stacked, w4, preferred_element_type=jnp.float32).astype(buf.dtype)
        for g in range(groups):
            side[j, :, g * LANES:(g + 1) * LANES] = y[g * rows:(g + 1) * rows]

    each_copy(step, step % 2, start)

    @pl.when(step == steps - 1)
    def _():
        each_copy(step - 1, (step + 1) % 2, wait)
        each_copy(step, step % 2, wait)


def transform_into_slots(three_center, coefficients, out_index, slot_index, group_slots):
    pair_count, rows, width = three_center.shape
    tile = coefficients.shape[1]
    steps = 8 if pair_count % 8 == 0 else 1
    per = pair_count // steps
    zeros = jnp.zeros_like(coefficients)
    w2 = jnp.concatenate(
        [
            jnp.concatenate([coefficients, zeros], axis=2),
            jnp.concatenate([zeros, coefficients], axis=2),
        ],
        axis=1,
    )
    grid_spec = pltpu.PrefetchScalarGridSpec(
        num_scalar_prefetch=2,
        grid=(steps,),
        in_specs=[
            pl.BlockSpec((per, rows, width), lambda i, o, s: (i, 0, 0)),
            pl.BlockSpec((per, 2 * tile, 2 * tile), lambda i, o, s: (i, 0, 0)),
        ],
        out_specs=[pl.BlockSpec(memory_space=pl.ANY)] * len(group_slots),
        scratch_shapes=[
            pltpu.VMEM((2, per, rows, width), three_center.dtype),
            pltpu.SemaphoreType.DMA((2, per)),
        ],
    )
    block_bytes = rows * width * 2
    return pl.pallas_call(
        _transform_kernel,
        grid_spec=grid_spec,
        out_shape=[jax.ShapeDtypeStruct((n, rows, width), three_center.dtype) for n in group_slots],
        compiler_params=pltpu.CompilerParams(dimension_semantics=("arbitrary",)),
        cost_estimate=pl.CostEstimate(
            flops=2 * pair_count * rows * width * 4 * tile,
            transcendentals=0,
            bytes_accessed=2 * pair_count * block_bytes,
        ),
    )(out_index, slot_index, three_center, w2)


def _gram_kernel(lab_ref, x_ref, o_ref, acc, fs):
    step = pl.program_id(0)
    half, cap = x_ref.shape[0], x_ref.shape[1]
    dom, rows, width = acc.shape
    block = o_ref.shape[0]

    @pl.when(step == 0)
    def _():
        acc[...] = jnp.zeros_like(acc)

    def accumulate(part):
        for s in range(half):
            for c in range(cap):
                e = lab_ref[(part * half + s) * cap + c]

                @pl.when(e >= 0)
                def _():
                    acc[e] += x_ref[s, c].astype(jnp.float32)

    @pl.when(step == 0)
    def _():
        accumulate(0)

    @pl.when(step == 1)
    def _():
        accumulate(1)
        fs[...] = acc[...].astype(fs.dtype).reshape(dom * rows, width)

    for part in range(2):
        @pl.when(step == part + 1)
        def _():
            lhs = fs[part * block:(part + 1) * block, :]
            o_ref[...] = lax.dot_general(
                lhs, fs[...], (((1,), (1,)), ((), ())), preferred_element_type=jnp.float32
            )


def domain_gram(received, labels, dom):
    sources, slots, rows, width = received.shape
    domain_rows = dom * rows
    half = sources // 2
    grid_spec = pltpu.PrefetchScalarGridSpec(
        num_scalar_prefetch=1,
        grid=(3,),
        in_specs=[pl.BlockSpec((half, CAP, rows, width), lambda i, lab: (jnp.minimum(i, 1), 0, 0, 0))],
        out_specs=pl.BlockSpec((domain_rows // 2, domain_rows), lambda i, lab: (jnp.maximum(i - 1, 0), 0)),
        scratch_shapes=[
            pltpu.VMEM((dom, rows, width), jnp.float32),
            pltpu.VMEM((domain_rows, width), received.dtype),
        ],
    )
    return pl.pallas_call(
        _gram_kernel,
        grid_spec=grid_spec,
        out_shape=jax.ShapeDtypeStruct((domain_rows, domain_rows), jnp.float32),
        compiler_params=pltpu.CompilerParams(
            dimension_semantics=("arbitrary",), vmem_limit_bytes=60 * 1024 * 1024
        ),
        cost_estimate=pl.CostEstimate(
            flops=2 * domain_rows * domain_rows * width,
            transcendentals=0,
            bytes_accessed=sources * slots * rows * width * 2 + domain_rows * domain_rows * 4,
        ),
    )(labels.reshape(-1), received)


def per_device(three_center, coefficients, target, domain_slot, owner_order):
    pair_count, tile_width, col_width = three_center.shape
    occ_count = lax.axis_size("occ")
    aux_count = lax.axis_size("aux")
    tile_count = owner_order.shape[0]
    owned_tiles = tile_count // occ_count
    slot_count = tile_count * CAP
    tile_ids = jnp.arange(tile_count, dtype=jnp.int32)
    pos = jnp.sum(jnp.where(owner_order[None, :] == target[:, None], tile_ids[None, :], 0), axis=1)
    pair_ids = jnp.arange(pair_count, dtype=jnp.int32)
    earlier = (target[:, None] == target[None, :]) & (pair_ids[:, None] > pair_ids[None, :])
    rank = jnp.sum(earlier.astype(jnp.int32), axis=1)
    out_index = pos % owned_tiles
    slot_index = (pos // owned_tiles) * CAP + rank
    tile_slot = out_index * occ_count * CAP + slot_index
    slot_ids = jnp.arange(slot_count, dtype=jnp.int32)
    labels = jnp.sum(jnp.where(tile_slot[None, :] == slot_ids[:, None], domain_slot[None, :] + 1, 0), axis=1) - 1
    labels = labels.reshape(owned_tiles, occ_count, CAP).transpose(1, 0, 2)
    received_labels = lax.all_to_all(labels, "occ", split_axis=0, concat_axis=0, tiled=True)

    buffers = transform_into_slots(
        three_center, coefficients, out_index, slot_index, [occ_count * CAP] * owned_tiles
    )
    pieces = []
    for k in range(owned_tiles):
        buffer = buffers[k].reshape(occ_count, CAP * tile_width, col_width)
        received = lax.all_to_all(buffer, "occ", split_axis=0, concat_axis=0, tiled=True)
        received = received.reshape(occ_count, CAP, tile_width, col_width)
        partial_gram = domain_gram(received, received_labels[:, k], DOM)
        pieces.append(lax.psum_scatter(partial_gram, "aux", scatter_dimension=0, tiled=True))
    return jnp.stack(pieces, axis=1)


def solution(mesh):
    in_specs = (P("occ", None, "aux"), P("occ", None, None), P("occ"), P("occ"), P())
    out_specs = P("aux", "occ", None)
    return jax.shard_map(
        per_device, mesh=mesh, in_specs=in_specs, out_specs=out_specs, check_vma=False
    )
```

```python
import functools
import math

import jax
import jax.numpy as jnp
from jax import lax
from jax.experimental import pallas as pl
from jax.experimental.pallas import tpu as pltpu
from jax.sharding import PartitionSpec as P

DOM = 16
CAP = 2
LANES = 256


def _transform_kernel(out_ref, slot_ref, tc_ref, w_ref, *rest):
    chunks = len(rest) - 2
    outs, (buf, sems) = rest[:chunks], rest[chunks:]
    step = pl.program_id(0)
    steps = pl.num_programs(0)
    per = tc_ref.shape[0]
    rows, width = tc_ref.shape[1], tc_ref.shape[2]
    groups = width // LANES
    half = w_ref.shape[1]
    side = buf.at[step % 2]

    def each_copy(at, parity, act):
        held = buf.at[parity]
        for j in range(per):
            chunk, local = out_ref[at * per + j], slot_ref[at * per + j]
            for kk in range(chunks):
                @pl.when(chunk == kk)
                def _():
                    act(pltpu.make_async_copy(held.at[j], outs[kk].at[local], sems.at[parity, j]))

    def start(cp):
        cp.start()

    def wait(cp):
        cp.wait()

    @pl.when(step >= 2)
    def _():
        each_copy(step - 2, step % 2, wait)

    pad = jnp.zeros((half, half), w_ref.dtype)
    for j in range(per):
        w2 = w_ref[j]
        w4 = jnp.concatenate(
            [jnp.concatenate([w2, pad], axis=1), jnp.concatenate([pad, w2], axis=1)], axis=0
        )
        x = tc_ref[j]
        stacked = jnp.concatenate([x[:, g * LANES:(g + 1) * LANES] for g in range(groups)], axis=0)
        y = jnp.dot(stacked, w4, preferred_element_type=jnp.float32).astype(buf.dtype)
        for g in range(groups):
            side[j, :, g * LANES:(g + 1) * LANES] = y[g * rows:(g + 1) * rows]

    each_copy(step, step % 2, start)

    @pl.when(step == steps - 1)
    def _():
        each_copy(step - 1, (step + 1) % 2, wait)
        each_copy(step, step % 2, wait)


def transform_into_slots(three_center, coefficients, out_index, slot_index, group_slots):
    pair_count, rows, width = three_center.shape
    tile = coefficients.shape[1]
    steps = 8 if pair_count % 8 == 0 else 1
    per = pair_count // steps
    zeros = jnp.zeros_like(coefficients)
    w2 = jnp.concatenate(
        [
            jnp.concatenate([coefficients, zeros], axis=2),
            jnp.concatenate([zeros, coefficients], axis=2),
        ],
        axis=1,
    )
    grid_spec = pltpu.PrefetchScalarGridSpec(
        num_scalar_prefetch=2,
        grid=(steps,),
        in_specs=[
            pl.BlockSpec((per, rows, width), lambda i, o, s: (i, 0, 0)),
            pl.BlockSpec((per, 2 * tile, 2 * tile), lambda i, o, s: (i, 0, 0)),
        ],
        out_specs=[pl.BlockSpec(memory_space=pl.ANY)] * len(group_slots),
        scratch_shapes=[
            pltpu.VMEM((2, per, rows, width), three_center.dtype),
            pltpu.SemaphoreType.DMA((2, per)),
        ],
    )
    block_bytes = rows * width * 2
    return pl.pallas_call(
        _transform_kernel,
        grid_spec=grid_spec,
        out_shape=[jax.ShapeDtypeStruct((n, rows, width), three_center.dtype) for n in group_slots],
        compiler_params=pltpu.CompilerParams(dimension_semantics=("arbitrary",)),
        cost_estimate=pl.CostEstimate(
            flops=2 * pair_count * rows * width * 4 * tile,
            transcendentals=0,
            bytes_accessed=2 * pair_count * block_bytes,
        ),
    )(out_index, slot_index, three_center, w2)


def _gram_kernel(lab_ref, x_ref, o_ref, acc, fs, *, tile, per_source):
    step = pl.program_id(0)
    half, cap = x_ref.shape[0], x_ref.shape[1]
    dom, rows, width = acc.shape
    block = o_ref.shape[0]

    @pl.when(step == 0)
    def _():
        acc[...] = jnp.zeros_like(acc)

    def accumulate(part):
        for s in range(half):
            for c in range(cap):
                e = lab_ref[(part * half + s) * per_source + tile * cap + c]

                @pl.when(e >= 0)
                def _():
                    acc[e] += x_ref[s, c].astype(jnp.float32)

    @pl.when(step == 0)
    def _():
        accumulate(0)

    @pl.when(step == 1)
    def _():
        accumulate(1)
        fs[...] = acc[...].astype(fs.dtype).reshape(dom * rows, width)

    for part in range(2):
        @pl.when(step == part + 1)
        def _():
            lhs = fs[part * block:(part + 1) * block, :]
            o_ref[...] = lax.dot_general(
                lhs, fs[...], (((1,), (1,)), ((), ())), preferred_element_type=jnp.float32
            )


def domain_gram(received, labels, dom, tile):
    sources, slots, rows, width = received.shape
    domain_rows = dom * rows
    half = sources // 2
    grid_spec = pltpu.PrefetchScalarGridSpec(
        num_scalar_prefetch=1,
        grid=(3,),
        in_specs=[pl.BlockSpec((half, CAP, rows, width), lambda i, lab: (jnp.minimum(i, 1), 0, 0, 0))],
        out_specs=pl.BlockSpec((domain_rows // 2, domain_rows), lambda i, lab: (jnp.maximum(i - 1, 0), 0)),
        scratch_shapes=[
            pltpu.VMEM((dom, rows, width), jnp.float32),
            pltpu.VMEM((domain_rows, width), received.dtype),
        ],
    )
    return pl.pallas_call(
        functools.partial(_gram_kernel, tile=tile, per_source=labels.size // sources),
        grid_spec=grid_spec,
        out_shape=jax.ShapeDtypeStruct((domain_rows, domain_rows), jnp.float32),
        compiler_params=pltpu.CompilerParams(
            dimension_semantics=("arbitrary",), vmem_limit_bytes=60 * 1024 * 1024
        ),
        cost_estimate=pl.CostEstimate(
            flops=2 * domain_rows * domain_rows * width,
            transcendentals=0,
            bytes_accessed=sources * slots * rows * width * 2 + domain_rows * domain_rows * 4,
        ),
    )(labels.reshape(-1), received)


def per_device(three_center, coefficients, target, domain_slot, owner_order):
    pair_count, tile_width, col_width = three_center.shape
    occ_count = lax.axis_size("occ")
    aux_count = lax.axis_size("aux")
    tile_count = owner_order.shape[0]
    owned_tiles = tile_count // occ_count
    slot_count = tile_count * CAP
    tile_ids = jnp.arange(tile_count, dtype=jnp.int32)
    pos = jnp.sum(jnp.where(owner_order[None, :] == target[:, None], tile_ids[None, :], 0), axis=1)
    pair_ids = jnp.arange(pair_count, dtype=jnp.int32)
    earlier = (target[:, None] == target[None, :]) & (pair_ids[:, None] > pair_ids[None, :])
    rank = jnp.sum(earlier.astype(jnp.int32), axis=1)
    out_index = pos % owned_tiles
    slot_index = (pos // owned_tiles) * CAP + rank
    tile_slot = out_index * occ_count * CAP + slot_index
    slot_ids = jnp.arange(slot_count, dtype=jnp.int32)
    labels = jnp.sum(jnp.where(tile_slot[None, :] == slot_ids[:, None], domain_slot[None, :] + 1, 0), axis=1) - 1
    labels = labels.reshape(owned_tiles, occ_count, CAP).transpose(1, 0, 2)
    received_labels = lax.all_to_all(labels, "occ", split_axis=0, concat_axis=0, tiled=True)

    buffers = transform_into_slots(
        three_center, coefficients, out_index, slot_index, [occ_count * CAP] * owned_tiles
    )
    pieces = []
    for k in range(owned_tiles):
        buffer = buffers[k].reshape(occ_count, CAP * tile_width, col_width)
        received = lax.all_to_all(buffer, "occ", split_axis=0, concat_axis=0, tiled=True)
        received = received.reshape(occ_count, CAP, tile_width, col_width)
        partial_gram = domain_gram(received, received_labels, DOM, k)
        pieces.append(lax.psum_scatter(partial_gram, "aux", scatter_dimension=0, tiled=True))
    return jnp.stack(pieces, axis=1)


def solution(mesh):
    in_specs = (P("occ", None, "aux"), P("occ", None, None), P("occ"), P("occ"), P())
    out_specs = P("aux", "occ", None)
    return jax.shard_map(
        per_device, mesh=mesh, in_specs=in_specs, out_specs=out_specs, check_vma=False
    )
```

```python
import functools
import math

import jax
import jax.numpy as jnp
from jax import lax
from jax.experimental import pallas as pl
from jax.experimental.pallas import tpu as pltpu
from jax.sharding import PartitionSpec as P

DOM = 16
CAP = 2
LANES = 256


def _transform_kernel(out_ref, slot_ref, tc_ref, w_ref, *rest):
    chunks = len(rest) - 2
    outs, (buf, sems) = rest[:chunks], rest[chunks:]
    step = pl.program_id(0)
    steps = pl.num_programs(0)
    per = tc_ref.shape[0]
    rows, width = tc_ref.shape[1], tc_ref.shape[2]
    groups = width // LANES
    half = w_ref.shape[1]
    side = buf.at[step % 2]

    def each_copy(at, parity, act):
        held = buf.at[parity]
        for j in range(per):
            chunk, local = out_ref[at * per + j], slot_ref[at * per + j]
            for kk in range(chunks):
                @pl.when(chunk == kk)
                def _():
                    act(pltpu.make_async_copy(held.at[j], outs[kk].at[local], sems.at[parity, j]))

    def start(cp):
        cp.start()

    def wait(cp):
        cp.wait()

    @pl.when(step >= 2)
    def _():
        each_copy(step - 2, step % 2, wait)

    pad = jnp.zeros((half, half), w_ref.dtype)
    for j in range(per):
        w2 = w_ref[j]
        w4 = jnp.concatenate(
            [jnp.concatenate([w2, pad], axis=1), jnp.concatenate([pad, w2], axis=1)], axis=0
        )
        x = tc_ref[j]
        stacked = jnp.concatenate([x[:, g * LANES:(g + 1) * LANES] for g in range(groups)], axis=0)
        y = jnp.dot(stacked, w4, preferred_element_type=jnp.float32).astype(buf.dtype)
        for g in range(groups):
            side[j, :, g * LANES:(g + 1) * LANES] = y[g * rows:(g + 1) * rows]

    each_copy(step, step % 2, start)

    @pl.when(step == steps - 1)
    def _():
        each_copy(step - 1, (step + 1) % 2, wait)
        each_copy(step, step % 2, wait)


def transform_into_slots(three_center, coefficients, out_index, slot_index, group_slots):
    pair_count, rows, width = three_center.shape
    tile = coefficients.shape[1]
    steps = 8 if pair_count % 8 == 0 else 1
    per = pair_count // steps
    zeros = jnp.zeros_like(coefficients)
    w2 = jnp.concatenate(
        [
            jnp.concatenate([coefficients, zeros], axis=2),
            jnp.concatenate([zeros, coefficients], axis=2),
        ],
        axis=1,
    )
    grid_spec = pltpu.PrefetchScalarGridSpec(
        num_scalar_prefetch=2,
        grid=(steps,),
        in_specs=[
            pl.BlockSpec((per, rows, width), lambda i, o, s: (i, 0, 0)),
            pl.BlockSpec((per, 2 * tile, 2 * tile), lambda i, o, s: (i, 0, 0)),
        ],
        out_specs=[pl.BlockSpec(memory_space=pl.ANY)] * len(group_slots),
        scratch_shapes=[
            pltpu.VMEM((2, per, rows, width), three_center.dtype),
            pltpu.SemaphoreType.DMA((2, per)),
        ],
    )
    block_bytes = rows * width * 2
    return pl.pallas_call(
        _transform_kernel,
        grid_spec=grid_spec,
        out_shape=[jax.ShapeDtypeStruct((n, rows, width), three_center.dtype) for n in group_slots],
        compiler_params=pltpu.CompilerParams(dimension_semantics=("arbitrary",)),
        cost_estimate=pl.CostEstimate(
            flops=2 * pair_count * rows * width * 4 * tile,
            transcendentals=0,
            bytes_accessed=2 * pair_count * block_bytes,
        ),
    )(out_index, slot_index, three_center, w2)


def _gram_kernel(lab_ref, x_ref, o_ref, acc, fs, *, tile, per_source):
    step = pl.program_id(0)
    half, cap = x_ref.shape[0], x_ref.shape[1]
    dom, rows, width = acc.shape
    block = o_ref.shape[0]

    @pl.when(step == 0)
    def _():
        acc[...] = jnp.zeros_like(acc)

    def accumulate(part):
        for s in range(half):
            for c in range(cap):
                e = lab_ref[(part * half + s) * per_source + tile * cap + c]

                @pl.when(e >= 0)
                def _():
                    acc[e] += x_ref[s, c].astype(jnp.float32)

    @pl.when(step == 0)
    def _():
        accumulate(0)

    @pl.when(step == 1)
    def _():
        accumulate(1)
        fs[...] = acc[...].astype(fs.dtype).reshape(dom * rows, width)

    for part in range(2):
        @pl.when(step == part + 1)
        def _():
            lhs = fs[part * block:(part + 1) * block, :]
            o_ref[...] = lax.dot_general(
                lhs, fs[...], (((1,), (1,)), ((), ())), preferred_element_type=jnp.float32
            )


def domain_gram(received, labels, dom, tile):
    sources, slots, rows, width = received.shape
    domain_rows = dom * rows
    half = sources // 2
    grid_spec = pltpu.PrefetchScalarGridSpec(
        num_scalar_prefetch=1,
        grid=(3,),
        in_specs=[pl.BlockSpec((half, CAP, rows, width), lambda i, lab: (jnp.minimum(i, 1), 0, 0, 0))],
        out_specs=pl.BlockSpec((domain_rows // 2, domain_rows), lambda i, lab: (jnp.maximum(i - 1, 0), 0)),
        scratch_shapes=[
            pltpu.VMEM((dom, rows, width), jnp.float32),
            pltpu.VMEM((domain_rows, width), received.dtype),
        ],
    )
    return pl.pallas_call(
        functools.partial(_gram_kernel, tile=tile, per_source=labels.size // sources),
        grid_spec=grid_spec,
        out_shape=jax.ShapeDtypeStruct((domain_rows, domain_rows), jnp.float32),
        compiler_params=pltpu.CompilerParams(
            dimension_semantics=("arbitrary",), vmem_limit_bytes=60 * 1024 * 1024
        ),
        cost_estimate=pl.CostEstimate(
            flops=2 * domain_rows * domain_rows * width,
            transcendentals=0,
            bytes_accessed=sources * slots * rows * width * 2 + domain_rows * domain_rows * 4,
        ),
    )(labels.reshape(-1), received)


def per_device(three_center, coefficients, target, domain_slot, owner_order):
    pair_count, tile_width, col_width = three_center.shape
    occ_count = lax.axis_size("occ")
    aux_count = lax.axis_size("aux")
    tile_count = owner_order.shape[0]
    owned_tiles = tile_count // occ_count
    slot_count = tile_count * CAP
    tile_ids = jnp.arange(tile_count, dtype=jnp.int32)
    pos = jnp.sum(jnp.where(owner_order[None, :] == target[:, None], tile_ids[None, :], 0), axis=1)
    pair_ids = jnp.arange(pair_count, dtype=jnp.int32)
    earlier = (target[:, None] == target[None, :]) & (pair_ids[:, None] > pair_ids[None, :])
    rank = jnp.sum(earlier.astype(jnp.int32), axis=1)
    out_index = pos % owned_tiles
    slot_index = (pos // owned_tiles) * CAP + rank
    tile_slot = out_index * occ_count * CAP + slot_index
    slot_ids = jnp.arange(slot_count, dtype=jnp.int32)
    labels = jnp.sum(jnp.where(tile_slot[None, :] == slot_ids[:, None], domain_slot[None, :] + 1, 0), axis=1) - 1
    labels = labels.reshape(owned_tiles, occ_count, CAP).transpose(1, 0, 2)

    labels, three_center = lax.optimization_barrier((labels, three_center))
    buffers = transform_into_slots(
        three_center, coefficients, out_index, slot_index, [occ_count * CAP] * owned_tiles
    )
    pieces = []
    for k in range(owned_tiles):
        buffer = buffers[k].reshape(occ_count, CAP * tile_width, col_width)
        received = lax.all_to_all(buffer, "occ", split_axis=0, concat_axis=0, tiled=True)
        if k == 0:
            labels, received = lax.optimization_barrier((labels, received))
            received_labels = lax.all_to_all(labels, "occ", split_axis=0, concat_axis=0, tiled=True)
        received = received.reshape(occ_count, CAP, tile_width, col_width)
        partial_gram = domain_gram(received, received_labels, DOM, k)
        pieces.append(lax.psum_scatter(partial_gram, "aux", scatter_dimension=0, tiled=True))
    return jnp.stack(pieces, axis=1)


def solution(mesh):
    in_specs = (P("occ", None, "aux"), P("occ", None, None), P("occ"), P("occ"), P())
    out_specs = P("aux", "occ", None)
    return jax.shard_map(
        per_device, mesh=mesh, in_specs=in_specs, out_specs=out_specs, check_vma=False
    )
```

```python
import functools
import math

import jax
import jax.numpy as jnp
from jax import lax
from jax.experimental import pallas as pl
from jax.experimental.pallas import tpu as pltpu
from jax.sharding import PartitionSpec as P

DOM = 16
CAP = 2
LANES = 256


def _transform_kernel(out_ref, slot_ref, tc_ref, w_ref, *rest):
    chunks = len(rest) - 2
    outs, (buf, sems) = rest[:chunks], rest[chunks:]
    step = pl.program_id(0)
    steps = pl.num_programs(0)
    per = tc_ref.shape[0]
    rows, width = tc_ref.shape[1], tc_ref.shape[2]
    groups = width // LANES
    half = w_ref.shape[1]
    side = buf.at[step % 2]

    def each_copy(at, parity, act):
        held = buf.at[parity]
        for j in range(per):
            chunk, local = out_ref[at * per + j], slot_ref[at * per + j]
            for kk in range(chunks):
                @pl.when(chunk == kk)
                def _():
                    act(pltpu.make_async_copy(held.at[j], outs[kk].at[local], sems.at[parity, j]))

    def start(cp):
        cp.start()

    def wait(cp):
        cp.wait()

    @pl.when(step >= 2)
    def _():
        each_copy(step - 2, step % 2, wait)

    pad = jnp.zeros((half, half), w_ref.dtype)
    for j in range(per):
        w2 = w_ref[j]
        w4 = jnp.concatenate(
            [jnp.concatenate([w2, pad], axis=1), jnp.concatenate([pad, w2], axis=1)], axis=0
        )
        x = tc_ref[j]
        stacked = jnp.concatenate([x[:, g * LANES:(g + 1) * LANES] for g in range(groups)], axis=0)
        y = jnp.dot(stacked, w4, preferred_element_type=jnp.float32).astype(buf.dtype)
        for g in range(groups):
            side[j, :, g * LANES:(g + 1) * LANES] = y[g * rows:(g + 1) * rows]

    each_copy(step, step % 2, start)

    @pl.when(step == steps - 1)
    def _():
        each_copy(step - 1, (step + 1) % 2, wait)
        each_copy(step, step % 2, wait)


def transform_into_slots(three_center, coefficients, out_index, slot_index, group_slots):
    pair_count, rows, width = three_center.shape
    tile = coefficients.shape[1]
    steps = 8 if pair_count % 8 == 0 else 1
    per = pair_count // steps
    zeros = jnp.zeros_like(coefficients)
    w2 = jnp.concatenate(
        [
            jnp.concatenate([coefficients, zeros], axis=2),
            jnp.concatenate([zeros, coefficients], axis=2),
        ],
        axis=1,
    )
    grid_spec = pltpu.PrefetchScalarGridSpec(
        num_scalar_prefetch=2,
        grid=(steps,),
        in_specs=[
            pl.BlockSpec((per, rows, width), lambda i, o, s: (i, 0, 0)),
            pl.BlockSpec((per, 2 * tile, 2 * tile), lambda i, o, s: (i, 0, 0)),
        ],
        out_specs=[pl.BlockSpec(memory_space=pl.ANY)] * len(group_slots),
        scratch_shapes=[
            pltpu.VMEM((2, per, rows, width), three_center.dtype),
            pltpu.SemaphoreType.DMA((2, per)),
        ],
    )
    block_bytes = rows * width * 2
    return pl.pallas_call(
        _transform_kernel,
        grid_spec=grid_spec,
        out_shape=[jax.ShapeDtypeStruct((n, rows, width), three_center.dtype) for n in group_slots],
        compiler_params=pltpu.CompilerParams(dimension_semantics=("arbitrary",)),
        cost_estimate=pl.CostEstimate(
            flops=2 * pair_count * rows * width * 4 * tile,
            transcendentals=0,
            bytes_accessed=2 * pair_count * block_bytes,
        ),
    )(out_index, slot_index, three_center, w2)


def _gram_kernel(lab_ref, x_ref, o_ref, acc, fs, *, tile, per_source):
    step = pl.program_id(0)
    half, cap = x_ref.shape[0], x_ref.shape[1]
    dom, rows, width = acc.shape
    block = o_ref.shape[0]

    @pl.when(step == 0)
    def _():
        acc[...] = jnp.zeros_like(acc)

    def accumulate(part):
        for s in range(half):
            for c in range(cap):
                e = lab_ref[(part * half + s) * per_source + tile * cap + c]

                @pl.when(e >= 0)
                def _():
                    acc[e] += x_ref[s, c].astype(jnp.float32)

    @pl.when(step == 0)
    def _():
        accumulate(0)

    @pl.when(step == 1)
    def _():
        accumulate(1)
        fs[...] = acc[...].astype(fs.dtype).reshape(dom * rows, width)

    for part in range(2):
        @pl.when(step == part + 1)
        def _():
            lhs = fs[part * block:(part + 1) * block, :]
            o_ref[...] = lax.dot_general(
                lhs, fs[...], (((1,), (1,)), ((), ())), preferred_element_type=jnp.float32
            )


def domain_gram(received, labels, dom, tile):
    sources, slots, rows, width = received.shape
    domain_rows = dom * rows
    half = sources // 2
    grid_spec = pltpu.PrefetchScalarGridSpec(
        num_scalar_prefetch=1,
        grid=(3,),
        in_specs=[pl.BlockSpec((half, CAP, rows, width), lambda i, lab: (jnp.minimum(i, 1), 0, 0, 0))],
        out_specs=pl.BlockSpec((domain_rows // 2, domain_rows), lambda i, lab: (jnp.maximum(i - 1, 0), 0)),
        scratch_shapes=[
            pltpu.VMEM((dom, rows, width), jnp.float32),
            pltpu.VMEM((domain_rows, width), received.dtype),
        ],
    )
    return pl.pallas_call(
        functools.partial(_gram_kernel, tile=tile, per_source=labels.size // sources),
        grid_spec=grid_spec,
        out_shape=jax.ShapeDtypeStruct((domain_rows, domain_rows), jnp.float32),
        compiler_params=pltpu.CompilerParams(
            dimension_semantics=("arbitrary",), vmem_limit_bytes=60 * 1024 * 1024
        ),
        cost_estimate=pl.CostEstimate(
            flops=2 * domain_rows * domain_rows * width,
            transcendentals=0,
            bytes_accessed=sources * slots * rows * width * 2 + domain_rows * domain_rows * 4,
        ),
    )(labels.reshape(-1), received)


def per_device(three_center, coefficients, target, domain_slot, owner_order):
    pair_count, tile_width, col_width = three_center.shape
    occ_count = lax.axis_size("occ")
    aux_count = lax.axis_size("aux")
    tile_count = owner_order.shape[0]
    owned_tiles = tile_count // occ_count
    slot_count = tile_count * CAP
    tile_ids = jnp.arange(tile_count, dtype=jnp.int32)
    pos = jnp.sum(jnp.where(owner_order[None, :] == target[:, None], tile_ids[None, :], 0), axis=1)
    pair_ids = jnp.arange(pair_count, dtype=jnp.int32)
    earlier = (target[:, None] == target[None, :]) & (pair_ids[:, None] > pair_ids[None, :])
    rank = jnp.sum(earlier.astype(jnp.int32), axis=1)
    out_index = pos % owned_tiles
    slot_index = (pos // owned_tiles) * CAP + rank
    tile_slot = out_index * occ_count * CAP + slot_index
    slot_ids = jnp.arange(slot_count, dtype=jnp.int32)
    labels = jnp.sum(jnp.where(tile_slot[None, :] == slot_ids[:, None], domain_slot[None, :] + 1, 0), axis=1) - 1
    labels = labels.reshape(owned_tiles, occ_count, CAP).transpose(1, 0, 2)

    received_labels = lax.all_to_all(labels, "occ", split_axis=0, concat_axis=0, tiled=True)
    label_table = received_labels.reshape(-1)
    label_table, three_center = lax.optimization_barrier((label_table, three_center))
    buffers = transform_into_slots(
        three_center, coefficients, out_index, slot_index, [occ_count * CAP] * owned_tiles
    )
    pieces = []
    for k in range(owned_tiles):
        buffer = buffers[k].reshape(occ_count, CAP * tile_width, col_width)
        received = lax.all_to_all(buffer, "occ", split_axis=0, concat_axis=0, tiled=True)
        received = received.reshape(occ_count, CAP, tile_width, col_width)
        partial_gram = domain_gram(received, label_table, DOM, k)
        pieces.append(lax.psum_scatter(partial_gram, "aux", scatter_dimension=0, tiled=True))
    return jnp.stack(pieces, axis=1)


def solution(mesh):
    in_specs = (P("occ", None, "aux"), P("occ", None, None), P("occ"), P("occ"), P())
    out_specs = P("aux", "occ", None)
    return jax.shard_map(
        per_device, mesh=mesh, in_specs=in_specs, out_specs=out_specs, check_vma=False
    )
```

```python
import functools
import math

import jax
import jax.numpy as jnp
from jax import lax
from jax.experimental import pallas as pl
from jax.experimental.pallas import tpu as pltpu
from jax.sharding import PartitionSpec as P

DOM = 16
CAP = 2
LANES = 256


def _transform_kernel(out_ref, slot_ref, tc_ref, w_ref, *rest):
    chunks = len(rest) - 2
    outs, (buf, sems) = rest[:chunks], rest[chunks:]
    step = pl.program_id(0)
    steps = pl.num_programs(0)
    per = tc_ref.shape[0]
    rows, width = tc_ref.shape[1], tc_ref.shape[2]
    groups = width // LANES
    half = w_ref.shape[1]
    side = buf.at[step % 2]

    def each_copy(at, parity, act):
        held = buf.at[parity]
        for j in range(per):
            chunk, local = out_ref[at * per + j], slot_ref[at * per + j]
            for kk in range(chunks):
                @pl.when(chunk == kk)
                def _():
                    act(pltpu.make_async_copy(held.at[j], outs[kk].at[local], sems.at[parity, j]))

    def start(cp):
        cp.start()

    def wait(cp):
        cp.wait()

    @pl.when(step >= 2)
    def _():
        each_copy(step - 2, step % 2, wait)

    pad = jnp.zeros((half, half), w_ref.dtype)
    for j in range(per):
        w2 = w_ref[j]
        w4 = jnp.concatenate(
            [jnp.concatenate([w2, pad], axis=1), jnp.concatenate([pad, w2], axis=1)], axis=0
        )
        x = tc_ref[j]
        stacked = jnp.concatenate([x[:, g * LANES:(g + 1) * LANES] for g in range(groups)], axis=0)
        y = jnp.dot(stacked, w4, preferred_element_type=jnp.float32).astype(buf.dtype)
        for g in range(groups):
            side[j, :, g * LANES:(g + 1) * LANES] = y[g * rows:(g + 1) * rows]

    each_copy(step, step % 2, start)

    @pl.when(step == steps - 1)
    def _():
        each_copy(step - 1, (step + 1) % 2, wait)
        each_copy(step, step % 2, wait)


def transform_into_slots(three_center, coefficients, out_index, slot_index, group_slots):
    pair_count, rows, width = three_center.shape
    tile = coefficients.shape[1]
    steps = 4 if pair_count % 4 == 0 else 1
    per = pair_count // steps
    zeros = jnp.zeros_like(coefficients)
    w2 = jnp.concatenate(
        [
            jnp.concatenate([coefficients, zeros], axis=2),
            jnp.concatenate([zeros, coefficients], axis=2),
        ],
        axis=1,
    )
    grid_spec = pltpu.PrefetchScalarGridSpec(
        num_scalar_prefetch=2,
        grid=(steps,),
        in_specs=[
            pl.BlockSpec((per, rows, width), lambda i, o, s: (i, 0, 0)),
            pl.BlockSpec((per, 2 * tile, 2 * tile), lambda i, o, s: (i, 0, 0)),
        ],
        out_specs=[pl.BlockSpec(memory_space=pl.ANY)] * len(group_slots),
        scratch_shapes=[
            pltpu.VMEM((2, per, rows, width), three_center.dtype),
            pltpu.SemaphoreType.DMA((2, per)),
        ],
    )
    block_bytes = rows * width * 2
    return pl.pallas_call(
        _transform_kernel,
        grid_spec=grid_spec,
        out_shape=[jax.ShapeDtypeStruct((n, rows, width), three_center.dtype) for n in group_slots],
        compiler_params=pltpu.CompilerParams(dimension_semantics=("arbitrary",)),
        cost_estimate=pl.CostEstimate(
            flops=2 * pair_count * rows * width * 4 * tile,
            transcendentals=0,
            bytes_accessed=2 * pair_count * block_bytes,
        ),
    )(out_index, slot_index, three_center, w2)


def _gram_kernel(lab_ref, x_ref, o_ref, acc, fs, *, tile, per_source):
    step = pl.program_id(0)
    half, cap = x_ref.shape[0], x_ref.shape[1]
    dom, rows, width = acc.shape
    block = o_ref.shape[0]

    @pl.when(step == 0)
    def _():
        acc[...] = jnp.zeros_like(acc)

    def accumulate(part):
        for s in range(half):
            for c in range(cap):
                e = lab_ref[(part * half + s) * per_source + tile * cap + c]

                @pl.when(e >= 0)
                def _():
                    acc[e] += x_ref[s, c].astype(jnp.float32)

    @pl.when(step == 0)
    def _():
        accumulate(0)

    @pl.when(step == 1)
    def _():
        accumulate(1)
        fs[...] = acc[...].astype(fs.dtype).reshape(dom * rows, width)

    for part in range(2):
        @pl.when(step == part + 1)
        def _():
            lhs = fs[part * block:(part + 1) * block, :]
            o_ref[...] = lax.dot_general(
                lhs, fs[...], (((1,), (1,)), ((), ())), preferred_element_type=jnp.float32
            )


def domain_gram(received, labels, dom, tile):
    sources, slots, rows, width = received.shape
    domain_rows = dom * rows
    half = sources // 2
    grid_spec = pltpu.PrefetchScalarGridSpec(
        num_scalar_prefetch=1,
        grid=(3,),
        in_specs=[pl.BlockSpec((half, CAP, rows, width), lambda i, lab: (jnp.minimum(i, 1), 0, 0, 0))],
        out_specs=pl.BlockSpec((domain_rows // 2, domain_rows), lambda i, lab: (jnp.maximum(i - 1, 0), 0)),
        scratch_shapes=[
            pltpu.VMEM((dom, rows, width), jnp.float32),
            pltpu.VMEM((domain_rows, width), received.dtype),
        ],
    )
    return pl.pallas_call(
        functools.partial(_gram_kernel, tile=tile, per_source=labels.size // sources),
        grid_spec=grid_spec,
        out_shape=jax.ShapeDtypeStruct((domain_rows, domain_rows), jnp.float32),
        compiler_params=pltpu.CompilerParams(
            dimension_semantics=("arbitrary",), vmem_limit_bytes=60 * 1024 * 1024
        ),
        cost_estimate=pl.CostEstimate(
            flops=2 * domain_rows * domain_rows * width,
            transcendentals=0,
            bytes_accessed=sources * slots * rows * width * 2 + domain_rows * domain_rows * 4,
        ),
    )(labels.reshape(-1), received)


def per_device(three_center, coefficients, target, domain_slot, owner_order):
    pair_count, tile_width, col_width = three_center.shape
    occ_count = lax.axis_size("occ")
    aux_count = lax.axis_size("aux")
    tile_count = owner_order.shape[0]
    owned_tiles = tile_count // occ_count
    slot_count = tile_count * CAP
    tile_ids = jnp.arange(tile_count, dtype=jnp.int32)
    pos = jnp.sum(jnp.where(owner_order[None, :] == target[:, None], tile_ids[None, :], 0), axis=1)
    pair_ids = jnp.arange(pair_count, dtype=jnp.int32)
    earlier = (target[:, None] == target[None, :]) & (pair_ids[:, None] > pair_ids[None, :])
    rank = jnp.sum(earlier.astype(jnp.int32), axis=1)
    out_index = pos % owned_tiles
    slot_index = (pos // owned_tiles) * CAP + rank
    tile_slot = out_index * occ_count * CAP + slot_index
    slot_ids = jnp.arange(slot_count, dtype=jnp.int32)
    labels = jnp.sum(jnp.where(tile_slot[None, :] == slot_ids[:, None], domain_slot[None, :] + 1, 0), axis=1) - 1
    labels = labels.reshape(owned_tiles, occ_count, CAP).transpose(1, 0, 2)

    received_labels = lax.all_to_all(labels, "occ", split_axis=0, concat_axis=0, tiled=True)
    label_table = received_labels.reshape(-1)
    label_table, three_center = lax.optimization_barrier((label_table, three_center))
    buffers = transform_into_slots(
        three_center, coefficients, out_index, slot_index, [occ_count * CAP] * owned_tiles
    )
    pieces = []
    for k in range(owned_tiles):
        buffer = buffers[k].reshape(occ_count, CAP * tile_width, col_width)
        received = lax.all_to_all(buffer, "occ", split_axis=0, concat_axis=0, tiled=True)
        received = received.reshape(occ_count, CAP, tile_width, col_width)
        partial_gram = domain_gram(received, label_table, DOM, k)
        pieces.append(lax.psum_scatter(partial_gram, "aux", scatter_dimension=0, tiled=True))
    return jnp.stack(pieces, axis=1)


def solution(mesh):
    in_specs = (P("occ", None, "aux"), P("occ", None, None), P("occ"), P("occ"), P())
    out_specs = P("aux", "occ", None)
    return jax.shard_map(
        per_device, mesh=mesh, in_specs=in_specs, out_specs=out_specs, check_vma=False
    )
```

```python
import functools
import math

import jax
import jax.numpy as jnp
from jax import lax
from jax.experimental import pallas as pl
from jax.experimental.pallas import tpu as pltpu
from jax.sharding import PartitionSpec as P

DOM = 16
CAP = 2
LANES = 256


def _transform_kernel(out_ref, slot_ref, tc_ref, w_ref, *rest):
    chunks = len(rest) - 2
    outs, (buf, sems) = rest[:chunks], rest[chunks:]
    step = pl.program_id(0)
    steps = pl.num_programs(0)
    per = tc_ref.shape[0]
    rows, width = tc_ref.shape[1], tc_ref.shape[2]
    groups = width // LANES
    half = w_ref.shape[1]
    side = buf.at[step % 2]

    def each_copy(at, parity, act):
        held = buf.at[parity]
        for j in range(per):
            chunk, local = out_ref[at * per + j], slot_ref[at * per + j]
            for kk in range(chunks):
                @pl.when(chunk == kk)
                def _():
                    act(pltpu.make_async_copy(held.at[j], outs[kk].at[local], sems.at[parity, j]))

    def start(cp):
        cp.start()

    def wait(cp):
        cp.wait()

    @pl.when(step >= 2)
    def _():
        each_copy(step - 2, step % 2, wait)

    pad = jnp.zeros((half, half), w_ref.dtype)
    for j in range(per):
        w2 = w_ref[j]
        w4 = jnp.concatenate(
            [jnp.concatenate([w2, pad], axis=1), jnp.concatenate([pad, w2], axis=1)], axis=0
        )
        x = tc_ref[j]
        stacked = jnp.concatenate([x[:, g * LANES:(g + 1) * LANES] for g in range(groups)], axis=0)
        y = jnp.dot(stacked, w4, preferred_element_type=jnp.float32).astype(buf.dtype)
        for g in range(groups):
            side[j, :, g * LANES:(g + 1) * LANES] = y[g * rows:(g + 1) * rows]

    each_copy(step, step % 2, start)

    @pl.when(step == steps - 1)
    def _():
        each_copy(step - 1, (step + 1) % 2, wait)
        each_copy(step, step % 2, wait)


def transform_into_slots(three_center, coefficients, out_index, slot_index, group_slots):
    pair_count, rows, width = three_center.shape
    tile = coefficients.shape[1]
    steps = 4 if pair_count % 4 == 0 else 1
    per = pair_count // steps
    zeros = jnp.zeros_like(coefficients)
    w2 = jnp.concatenate(
        [
            jnp.concatenate([coefficients, zeros], axis=2),
            jnp.concatenate([zeros, coefficients], axis=2),
        ],
        axis=1,
    )
    grid_spec = pltpu.PrefetchScalarGridSpec(
        num_scalar_prefetch=2,
        grid=(steps,),
        in_specs=[
            pl.BlockSpec((per, rows, width), lambda i, o, s: (i, 0, 0)),
            pl.BlockSpec((per, 2 * tile, 2 * tile), lambda i, o, s: (i, 0, 0)),
        ],
        out_specs=[pl.BlockSpec(memory_space=pl.ANY)] * len(group_slots),
        scratch_shapes=[
            pltpu.VMEM((2, per, rows, width), three_center.dtype),
            pltpu.SemaphoreType.DMA((2, per)),
        ],
    )
    block_bytes = rows * width * 2
    return pl.pallas_call(
        _transform_kernel,
        grid_spec=grid_spec,
        out_shape=[jax.ShapeDtypeStruct((n, rows, width), three_center.dtype) for n in group_slots],
        compiler_params=pltpu.CompilerParams(dimension_semantics=("arbitrary",)),
        cost_estimate=pl.CostEstimate(
            flops=2 * pair_count * rows * width * 4 * tile,
            transcendentals=0,
            bytes_accessed=2 * pair_count * block_bytes,
        ),
    )(out_index, slot_index, three_center, w2)


def _gram_kernel(lab_ref, x_ref, o_ref, acc, fs, *, tile, per_source):
    step = pl.program_id(0)
    half, cap = x_ref.shape[0], x_ref.shape[1]
    dom, rows, width = acc.shape
    block = o_ref.shape[0]

    @pl.when(step == 0)
    def _():
        acc[...] = jnp.zeros_like(acc)

    def accumulate(part):
        for s in range(half):
            for c in range(cap):
                e = lab_ref[(part * half + s) * per_source + tile * cap + c]

                @pl.when(e >= 0)
                def _():
                    acc[e] += x_ref[s, c].astype(jnp.float32)

    @pl.when(step == 0)
    def _():
        accumulate(0)

    @pl.when(step == 1)
    def _():
        accumulate(1)
        fs[...] = acc[...].astype(fs.dtype).reshape(dom * rows, width)

    for part in range(2):
        @pl.when(step == part + 1)
        def _():
            lhs = fs[part * block:(part + 1) * block, :]
            o_ref[...] = lax.dot_general(
                lhs, fs[...], (((1,), (1,)), ((), ())), preferred_element_type=jnp.float32
            )


def domain_gram(received, labels, dom, tile):
    sources, slots, rows, width = received.shape
    domain_rows = dom * rows
    half = sources // 2
    grid_spec = pltpu.PrefetchScalarGridSpec(
        num_scalar_prefetch=1,
        grid=(3,),
        in_specs=[pl.BlockSpec((half, CAP, rows, width), lambda i, lab: (jnp.minimum(i, 1), 0, 0, 0))],
        out_specs=pl.BlockSpec((domain_rows // 2, domain_rows), lambda i, lab: (jnp.maximum(i - 1, 0), 0)),
        scratch_shapes=[
            pltpu.VMEM((dom, rows, width), jnp.float32),
            pltpu.VMEM((domain_rows, width), received.dtype),
        ],
    )
    return pl.pallas_call(
        functools.partial(_gram_kernel, tile=tile, per_source=labels.size // sources),
        grid_spec=grid_spec,
        out_shape=jax.ShapeDtypeStruct((domain_rows, domain_rows), jnp.float32),
        compiler_params=pltpu.CompilerParams(
            dimension_semantics=("arbitrary",), vmem_limit_bytes=60 * 1024 * 1024
        ),
        cost_estimate=pl.CostEstimate(
            flops=2 * domain_rows * domain_rows * width,
            transcendentals=0,
            bytes_accessed=sources * slots * rows * width * 2 + domain_rows * domain_rows * 4,
        ),
    )(labels.reshape(-1), received)


def per_device(three_center, coefficients, target, domain_slot, owner_order):
    pair_count, tile_width, col_width = three_center.shape
    occ_count = lax.axis_size("occ")
    aux_count = lax.axis_size("aux")
    tile_count = owner_order.shape[0]
    owned_tiles = tile_count // occ_count
    slot_count = tile_count * CAP
    tile_ids = jnp.arange(tile_count, dtype=jnp.int32)
    pos = jnp.sum(jnp.where(owner_order[None, :] == target[:, None], tile_ids[None, :], 0), axis=1)
    pair_ids = jnp.arange(pair_count, dtype=jnp.int32)
    earlier = (target[:, None] == target[None, :]) & (pair_ids[:, None] > pair_ids[None, :])
    rank = jnp.sum(earlier.astype(jnp.int32), axis=1)
    out_index = pos % owned_tiles
    slot_index = (pos // owned_tiles) * CAP + rank
    tile_slot = out_index * occ_count * CAP + slot_index
    slot_ids = jnp.arange(slot_count, dtype=jnp.int32)
    labels = jnp.sum(jnp.where(tile_slot[None, :] == slot_ids[:, None], domain_slot[None, :] + 1, 0), axis=1) - 1
    labels = labels.reshape(owned_tiles, occ_count, CAP).transpose(1, 0, 2)

    received_labels = lax.all_to_all(labels, "occ", split_axis=0, concat_axis=0, tiled=True)
    label_table = received_labels.reshape(-1)
    label_table, three_center = lax.optimization_barrier((label_table, three_center))
    buffers = transform_into_slots(
        three_center, coefficients, out_index, slot_index, [occ_count * CAP] * owned_tiles
    )
    pieces = []
    for k in range(owned_tiles):
        buffer = buffers[k].reshape(occ_count, CAP * tile_width, col_width)
        received = lax.all_to_all(buffer, "occ", split_axis=0, concat_axis=0, tiled=True)
        received = received.reshape(occ_count, CAP, tile_width, col_width)
        partial_gram = domain_gram(received, label_table, DOM, k)
        pieces.append(lax.psum_scatter(partial_gram, "aux", scatter_dimension=0, tiled=True))
    return jnp.concatenate(pieces, axis=1).reshape(pieces[0].shape[0], owned_tiles, -1)


def solution(mesh):
    in_specs = (P("occ", None, "aux"), P("occ", None, None), P("occ"), P("occ"), P())
    out_specs = P("aux", "occ", None)
    return jax.shard_map(
        per_device, mesh=mesh, in_specs=in_specs, out_specs=out_specs, check_vma=False
    )
```

```python
import functools
import math

import jax
import jax.numpy as jnp
from jax import lax
from jax.experimental import pallas as pl
from jax.experimental.pallas import tpu as pltpu
from jax.sharding import PartitionSpec as P

DOM = 16
CAP = 2
LANES = 256


def _transform_kernel(out_ref, slot_ref, tc_ref, w_ref, *rest):
    chunks = len(rest) - 2
    outs, (buf, sems) = rest[:chunks], rest[chunks:]
    step = pl.program_id(0)
    steps = pl.num_programs(0)
    per = tc_ref.shape[0]
    rows, width = tc_ref.shape[1], tc_ref.shape[2]
    groups = width // LANES
    half = w_ref.shape[1]
    side = buf.at[step % 2]

    def each_copy(at, parity, act):
        held = buf.at[parity]
        for j in range(per):
            chunk, local = out_ref[at * per + j], slot_ref[at * per + j]
            for kk in range(chunks):
                @pl.when(chunk == kk)
                def _():
                    act(pltpu.make_async_copy(held.at[j], outs[kk].at[local], sems.at[parity, j]))

    def start(cp):
        cp.start()

    def wait(cp):
        cp.wait()

    @pl.when(step >= 2)
    def _():
        each_copy(step - 2, step % 2, wait)

    pad = jnp.zeros((half, half), w_ref.dtype)
    for j in range(per):
        w2 = w_ref[j]
        w4 = jnp.concatenate(
            [jnp.concatenate([w2, pad], axis=1), jnp.concatenate([pad, w2], axis=1)], axis=0
        )
        x = tc_ref[j]
        stacked = jnp.concatenate([x[:, g * LANES:(g + 1) * LANES] for g in range(groups)], axis=0)
        y = jnp.dot(stacked, w4, preferred_element_type=jnp.float32).astype(buf.dtype)
        for g in range(groups):
            side[j, :, g * LANES:(g + 1) * LANES] = y[g * rows:(g + 1) * rows]

    each_copy(step, step % 2, start)

    @pl.when(step == steps - 1)
    def _():
        each_copy(step - 1, (step + 1) % 2, wait)
        each_copy(step, step % 2, wait)


def transform_into_slots(three_center, coefficients, out_index, slot_index, group_slots):
    pair_count, rows, width = three_center.shape
    tile = coefficients.shape[1]
    steps = 3 if pair_count % 3 == 0 else 1
    per = pair_count // steps
    zeros = jnp.zeros_like(coefficients)
    w2 = jnp.concatenate(
        [
            jnp.concatenate([coefficients, zeros], axis=2),
            jnp.concatenate([zeros, coefficients], axis=2),
        ],
        axis=1,
    )
    grid_spec = pltpu.PrefetchScalarGridSpec(
        num_scalar_prefetch=2,
        grid=(steps,),
        in_specs=[
            pl.BlockSpec((per, rows, width), lambda i, o, s: (i, 0, 0)),
            pl.BlockSpec((per, 2 * tile, 2 * tile), lambda i, o, s: (i, 0, 0)),
        ],
        out_specs=[pl.BlockSpec(memory_space=pl.ANY)] * len(group_slots),
        scratch_shapes=[
            pltpu.VMEM((2, per, rows, width), three_center.dtype),
            pltpu.SemaphoreType.DMA((2, per)),
        ],
    )
    block_bytes = rows * width * 2
    return pl.pallas_call(
        _transform_kernel,
        grid_spec=grid_spec,
        out_shape=[jax.ShapeDtypeStruct((n, rows, width), three_center.dtype) for n in group_slots],
        compiler_params=pltpu.CompilerParams(dimension_semantics=("arbitrary",)),
        cost_estimate=pl.CostEstimate(
            flops=2 * pair_count * rows * width * 4 * tile,
            transcendentals=0,
            bytes_accessed=2 * pair_count * block_bytes,
        ),
    )(out_index, slot_index, three_center, w2)


def _gram_kernel(lab_ref, x_ref, o_ref, acc, fs, *, tile, per_source):
    step = pl.program_id(0)
    half, cap = x_ref.shape[0], x_ref.shape[1]
    dom, rows, width = acc.shape
    block = o_ref.shape[0]

    @pl.when(step == 0)
    def _():
        acc[...] = jnp.zeros_like(acc)

    def accumulate(part):
        for s in range(half):
            for c in range(cap):
                e = lab_ref[(part * half + s) * per_source + tile * cap + c]

                @pl.when(e >= 0)
                def _():
                    acc[e] += x_ref[s, c].astype(jnp.float32)

    @pl.when(step == 0)
    def _():
        accumulate(0)

    @pl.when(step == 1)
    def _():
        accumulate(1)
        fs[...] = acc[...].astype(fs.dtype).reshape(dom * rows, width)

    for part in range(2):
        @pl.when(step == part + 1)
        def _():
            lhs = fs[part * block:(part + 1) * block, :]
            o_ref[...] = lax.dot_general(
                lhs, fs[...], (((1,), (1,)), ((), ())), preferred_element_type=jnp.float32
            )


def domain_gram(received, labels, dom, tile):
    sources, slots, rows, width = received.shape
    domain_rows = dom * rows
    half = sources // 2
    grid_spec = pltpu.PrefetchScalarGridSpec(
        num_scalar_prefetch=1,
        grid=(3,),
        in_specs=[pl.BlockSpec((half, CAP, rows, width), lambda i, lab: (jnp.minimum(i, 1), 0, 0, 0))],
        out_specs=pl.BlockSpec((domain_rows // 2, domain_rows), lambda i, lab: (jnp.maximum(i - 1, 0), 0)),
        scratch_shapes=[
            pltpu.VMEM((dom, rows, width), jnp.float32),
            pltpu.VMEM((domain_rows, width), received.dtype),
        ],
    )
    return pl.pallas_call(
        functools.partial(_gram_kernel, tile=tile, per_source=labels.size // sources),
        grid_spec=grid_spec,
        out_shape=jax.ShapeDtypeStruct((domain_rows, domain_rows), jnp.float32),
        compiler_params=pltpu.CompilerParams(
            dimension_semantics=("arbitrary",), vmem_limit_bytes=60 * 1024 * 1024
        ),
        cost_estimate=pl.CostEstimate(
            flops=2 * domain_rows * domain_rows * width,
            transcendentals=0,
            bytes_accessed=sources * slots * rows * width * 2 + domain_rows * domain_rows * 4,
        ),
    )(labels.reshape(-1), received)


def per_device(three_center, coefficients, target, domain_slot, owner_order):
    pair_count, tile_width, col_width = three_center.shape
    occ_count = lax.axis_size("occ")
    aux_count = lax.axis_size("aux")
    tile_count = owner_order.shape[0]
    owned_tiles = tile_count // occ_count
    slot_count = tile_count * CAP
    tile_ids = jnp.arange(tile_count, dtype=jnp.int32)
    pos = jnp.sum(jnp.where(owner_order[None, :] == target[:, None], tile_ids[None, :], 0), axis=1)
    pair_ids = jnp.arange(pair_count, dtype=jnp.int32)
    earlier = (target[:, None] == target[None, :]) & (pair_ids[:, None] > pair_ids[None, :])
    rank = jnp.sum(earlier.astype(jnp.int32), axis=1)
    out_index = pos % owned_tiles
    slot_index = (pos // owned_tiles) * CAP + rank
    tile_slot = out_index * occ_count * CAP + slot_index
    slot_ids = jnp.arange(slot_count, dtype=jnp.int32)
    labels = jnp.sum(jnp.where(tile_slot[None, :] == slot_ids[:, None], domain_slot[None, :] + 1, 0), axis=1) - 1
    labels = labels.reshape(owned_tiles, occ_count, CAP).transpose(1, 0, 2)

    received_labels = lax.all_to_all(labels, "occ", split_axis=0, concat_axis=0, tiled=True)
    label_table = received_labels.reshape(-1)
    label_table, three_center = lax.optimization_barrier((label_table, three_center))
    buffers = transform_into_slots(
        three_center, coefficients, out_index, slot_index, [occ_count * CAP] * owned_tiles
    )
    pieces = []
    for k in range(owned_tiles):
        buffer = buffers[k].reshape(occ_count, CAP * tile_width, col_width)
        received = lax.all_to_all(buffer, "occ", split_axis=0, concat_axis=0, tiled=True)
        received = received.reshape(occ_count, CAP, tile_width, col_width)
        partial_gram = domain_gram(received, label_table, DOM, k)
        pieces.append(lax.psum_scatter(partial_gram, "aux", scatter_dimension=0, tiled=True))
    return jnp.concatenate(pieces, axis=1).reshape(pieces[0].shape[0], owned_tiles, -1)


def solution(mesh):
    in_specs = (P("occ", None, "aux"), P("occ", None, None), P("occ"), P("occ"), P())
    out_specs = P("aux", "occ", None)
    return jax.shard_map(
        per_device, mesh=mesh, in_specs=in_specs, out_specs=out_specs, check_vma=False
    )
```
